32 devices in a mesh: groups: 2 (over x), height: 16 (over z, y, core).
Axes of the slice: x: 2, y: 2, z: 4, core: 2. Of those that a mesh axis runs over, the one named last changes fastest.
Arguments:
- latent: bfloat16 [3, 64, 80, 512], P(None, ('groups', 'height')), parts along dimension 1, may hold values from -120 to 120
- gain_first: float32 [512], replicated, may hold values from 0.1 to 1.9
- shift_first: float32 [512], replicated, may hold values from -3 to 3
- kernel_first: bfloat16 [27, 512, 512], P(None, 'height'), may hold values from -0.0546875 to 0.0546875
- bias_first: float32 [512], replicated, may hold values from -2 to 2
- gain_second: float32 [512], replicated, may hold values from 0.1 to 1.9
- shift_second: float32 [512], replicated, may hold values from -3 to 3
- kernel_second: bfloat16 [27, 512, 512], P(None, 'height'), may hold values from -0.0546875 to 0.0546875
- bias_second: float32 [512], replicated, may hold values from -2 to 2
Outputs:
- upsampled: bfloat16 [3, 128, 160, 512], P(None, ('groups', 'height')), parts along dimension 1
The draws below stay inside these ranges and needn't reach their ends.
There are 2 independent parts, one for each index of `groups`. The reference program is written for one: setup_inputs(seed, part) draws one part's arguments, and reference() takes and returns one part's arrays. A program takes and returns all parts, laid end to end along the dimension named above; an argument that names none is the same for every part. Nothing has to cross between parts.
All inputs are finite; a program needn't handle non-finite values.
Results may differ from the reference program's by a relative error of at most 0.0045.
Values may be sent and summed in bfloat16 or wider, within the bound.
No kernel may reach another device: no remote copies, remote signals or barrier semaphores. Data moves between devices by JAX's collectives and lax.ppermute only.
A program may use at most 128 MiB of HBM per device.

```python
import math
import jax
import jax.numpy as jnp
from jax import lax

C = 512
GROUPS = 32
FRAMES = 3
W = 80
H = 32


def draw_latent(key, part):
    keyed = jax.random.fold_in(key, 11)
    key_noise, key_rows, key_chans = jax.random.split(keyed, 3)
    noise = jnp.clip(jax.random.normal(key_noise, (FRAMES, H, W, C), jnp.float32), -6.0, 6.0)
    position = jnp.arange(H, dtype=jnp.float32) / max(H - 1, 1)
    row_scale = jnp.exp(position * math.log(3.0) + jax.random.uniform(key_rows, (H,), jnp.float32, -0.69, 0.69))
    chan_scale = jnp.exp(jax.random.uniform(key_chans, (C,), jnp.float32, math.log(0.3), math.log(3.0)))
    values = noise * row_scale[None, :, None, None] * chan_scale[None, None, None, :]
    return values.astype(jnp.bfloat16)


def steps_of(key, dims, cuts, low, top_value):
    def one(dim, shards_of):
        steps = jax.random.uniform(jax.random.fold_in(jax.random.fold_in(key, 6), dim), (shards_of,), jnp.float32, low / len(cuts), top_value / len(cuts))
        return jnp.repeat(jnp.exp(steps), dims[dim] // shards_of).reshape((-1,) + (1,) * (len(dims) - dim - 1))

    factor_of = one(*cuts[0])
    for cut in cuts[1:]:
        factor_of = factor_of * one(*cut)
    return factor_of


def normal_values(rng, shape, spread, limit, cuts=(), kind=jnp.bfloat16):
    loudness = steps_of(rng, shape, cuts, -0.22, 0.18) if cuts else 1.0
    result = jax.random.normal(rng, shape, jnp.float32) * spread * loudness
    return jnp.minimum(jnp.maximum(result, -limit), limit).astype(kind)


def setup_inputs(seed: int = 0, part: int = 0) -> dict:
    keys = jax.random.split(jax.random.key(seed), 10)
    own_keys = jax.random.split(jax.random.fold_in(keys[9], part), 10)
    latent = draw_latent(jax.random.fold_in(jax.random.fold_in(keys[9], part), 71), part)
    gain_first = jnp.clip(1.0 + 0.18 * jax.random.normal(keys[1], (C,), jnp.float32), 0.1, 1.9)
    shift_first = normal_values(keys[2], (C,), 0.5, 3.0, (), jnp.float32)
    kernel_first = normal_values(keys[3], (27, C, C), (27 * C) ** -0.5, 0.0546875, ((1, 16),))
    bias_first = normal_values(keys[4], (C,), 0.3, 2.0, (), jnp.float32)
    gain_second = jnp.clip(1.0 + 0.18 * jax.random.normal(keys[5], (C,), jnp.float32), 0.1, 1.9)
    shift_second = normal_values(keys[6], (C,), 0.5, 3.0, (), jnp.float32)
    kernel_second = normal_values(keys[7], (27, C, C), (27 * C) ** -0.5, 0.0546875, ((1, 16),))
    bias_second = normal_values(keys[8], (C,), 0.3, 2.0, (), jnp.float32)
    return {"latent": latent, "gain_first": gain_first, "shift_first": shift_first, "kernel_first": kernel_first, "bias_first": bias_first, "gain_second": gain_second, "shift_second": shift_second, "kernel_second": kernel_second, "bias_second": bias_second}


def group_act(field, norm_gain, norm_shift):
    values = field.astype(jnp.float32)
    frame_total, row_total, col_total, chan_total = values.shape
    grouped = values.reshape(frame_total, row_total, col_total, GROUPS, chan_total // GROUPS)
    group_mean = lax.optimization_barrier(jnp.mean(grouped, axis=(0, 1, 2, 4)))
    centred = grouped - group_mean[:, None]
    variance = lax.optimization_barrier(jnp.mean(centred * centred, axis=(0, 1, 2, 4)))
    normed = centred * lax.rsqrt(variance + 1e-06)[:, None]
    normed = normed.reshape(frame_total, row_total, col_total, chan_total) * norm_gain + norm_shift
    return jax.nn.silu(normed).astype(jnp.bfloat16)

def causal_conv(active, kernel, bias):
    frame_total, row_total, col_total, chan_total = active.shape
    leading = jnp.concatenate([active[:1], active[:1], active], axis=0)
    padded = jnp.pad(leading, ((0, 0), (1, 1), (1, 1), (0, 0)))
    summed = jnp.zeros((frame_total * row_total * col_total, kernel.shape[2]), jnp.float32)
    for step_t in range(3):
        for step_h in range(3):
            for step_w in range(3):
                window = padded[step_t:step_t + frame_total, step_h:step_h + row_total, step_w:step_w + col_total]
                summed = summed + jnp.dot(window.reshape(-1, chan_total), kernel[9 * step_t + 3 * step_h + step_w], preferred_element_type=jnp.float32)
    return summed.reshape(frame_total, row_total, col_total, -1) + bias

def reference(latent, gain_first, shift_first, kernel_first, bias_first, gain_second, shift_second, kernel_second, bias_second):
    act_first = group_act(latent, gain_first, shift_first)
    hidden = causal_conv(act_first, kernel_first, bias_first).astype(jnp.bfloat16)
    act_second = group_act(hidden, gain_second, shift_second)
    branch = causal_conv(act_second, kernel_second, bias_second)
    summed = (latent.astype(jnp.float32) + branch).astype(jnp.bfloat16)
    return jnp.repeat(jnp.repeat(summed, 2, axis=1), 2, axis=2)
```

```python
import jax
import jax.numpy as jnp
from jax import lax
from jax.sharding import Mesh
from jax.sharding import PartitionSpec as P

GROUPS = 32
CHAN_BLOCKS = 4
EPS = 1e-06


def shift_pairs(count, step):
    return [(i, (i + step) % count) for i in range(count)]


def butterfly_stats(sums, squares, count, axes):
    for axis in axes:
        size = lax.axis_size(axis)
        bit = 1
        while bit < size:
            pairs = [(i, i ^ bit) for i in range(size)]
            other_sums, other_squares = lax.ppermute((sums, squares), axis, pairs)
            gap = sums - other_sums
            squares = (squares + other_squares) + gap * gap / (2.0 * count)
            sums = sums + other_sums
            count = count * 2
            bit *= 2
    return sums, squares, count


def local_stats(values, groups):
    frames, rows, cols, chans = values.shape
    grouped = values.reshape(frames * rows * cols, groups, chans // groups)
    count = float(frames * rows * cols * (chans // groups))
    sums = jnp.sum(grouped, axis=(0, 2))
    centred = grouped - (sums / count)[None, :, None]
    squares = jnp.sum(centred * centred, axis=(0, 2))
    return sums, squares, count


def group_scale(sums, squares, count, group_size):
    mean = sums / count
    scale = lax.rsqrt(squares / count + EPS)
    return jnp.repeat(mean, group_size), jnp.repeat(scale, group_size)


def activate(values, mean_chan, scale_chan, gain, shift):
    normed = (values - mean_chan) * scale_chan * gain + shift
    return jax.nn.silu(normed).astype(jnp.bfloat16)


def gather_blocks(block, axis_name, dim, total):
    size = lax.axis_size(axis_name)
    me = lax.axis_index(axis_name)
    width = block.shape[dim]
    shape = list(block.shape)
    shape[dim] = total
    out = jnp.zeros(shape, block.dtype)
    for step in range(size):
        piece = block if step == 0 else lax.ppermute(block, axis_name, shift_pairs(size, step))
        source = (me - step) % size
        start = [0] * len(shape)
        start[dim] = source * width
        out = lax.dynamic_update_slice(out, piece, start)
    return out


def with_row_halo(cells, axis_name):
    size = lax.axis_size(axis_name)
    down = [(i, i + 1) for i in range(size - 1)]
    up = [(i + 1, i) for i in range(size - 1)]
    top = lax.ppermute(cells[:, -1:], axis_name, down)
    bottom = lax.ppermute(cells[:, :1], axis_name, up)
    return jnp.concatenate([top, cells, bottom], axis=1)


def causal_conv(extended, kernel, bias):
    leading = jnp.concatenate([extended[:1], extended[:1], extended], axis=0)
    taps, chans, outs = kernel.shape
    weights = kernel.reshape(3, 3, 3, chans, outs)
    summed = lax.conv_general_dilated(
        leading[None],
        weights,
        window_strides=(1, 1, 1),
        padding=((0, 0), (0, 0), (1, 1)),
        dimension_numbers=("NDHWC", "DHWIO", "NDHWC"),
        preferred_element_type=jnp.float32,
    )
    return summed[0] + bias


def kernel_block(shard, chans):
    size = lax.axis_size("hq")
    me = lax.axis_index("hq")
    taps, in_block, outs = shard.shape
    width = outs // size
    out = jnp.zeros((taps, in_block * size, width), shard.dtype)
    for step in range(size):
        target = (me + step) % size
        piece = lax.dynamic_slice_in_dim(shard, target * width, width, axis=2)
        if step:
            piece = lax.ppermute(piece, "hq", shift_pairs(size, step))
        source = (me - step) % size
        out = lax.dynamic_update_slice(out, piece, (0, source * in_block, 0))
    return lax.all_gather(out, "hz", axis=1, tiled=True)


def scatter_rows(branch, slab_rows, chans):
    size = lax.axis_size("hq")
    me = lax.axis_index("hq")
    frames, rows, cols, width = branch.shape
    out = jnp.zeros((frames, slab_rows, cols, chans), branch.dtype)
    for step in range(size):
        target = (me + step) % size
        piece = lax.dynamic_slice_in_dim(branch, target * slab_rows, slab_rows, axis=1)
        if step:
            piece = lax.ppermute(piece, "hq", shift_pairs(size, step))
        source = (me - step) % size
        out = lax.dynamic_update_slice(out, piece, (0, 0, 0, source * width))
    return out


def per_device(
    latent,
    gain_first,
    shift_first,
    kernel_first,
    bias_first,
    gain_second,
    shift_second,
    kernel_second,
    bias_second,
):
    frames, slab_rows, cols, chans = latent.shape
    blocks = lax.axis_size("hq")
    width = chans // blocks
    me = lax.axis_index("hq")
    group_size = chans // GROUPS

    weights_first = kernel_block(kernel_first, chans)
    weights_second = kernel_block(kernel_second, chans)

    values = latent.astype(jnp.float32)
    sums, squares, count = local_stats(values, GROUPS)
    sums, squares, count = butterfly_stats(sums, squares, count, ("hq", "hz"))
    mean_chan, scale_chan = group_scale(sums, squares, count, group_size)
    act_first = activate(values, mean_chan, scale_chan, gain_first, shift_first)

    group_rows = gather_blocks(act_first, "hq", 1, slab_rows * blocks)
    extended = with_row_halo(group_rows, "hz")
    own_bias = lax.dynamic_slice_in_dim(bias_first, me * width, width)
    hidden = causal_conv(extended, weights_first, own_bias).astype(jnp.bfloat16)

    hidden_values = hidden.astype(jnp.float32)
    sums, squares, count = local_stats(hidden_values, width // group_size)
    sums, squares, count = butterfly_stats(sums, squares, count, ("hz",))
    mean_own, scale_own = group_scale(sums, squares, count, group_size)
    own_gain = lax.dynamic_slice_in_dim(gain_second, me * width, width)
    own_shift = lax.dynamic_slice_in_dim(shift_second, me * width, width)
    act_second = activate(hidden_values, mean_own, scale_own, own_gain, own_shift)

    extended_next = with_row_halo(act_second, "hz")
    extended_next = gather_blocks(extended_next, "hq", 3, chans)
    own_bias_next = lax.dynamic_slice_in_dim(bias_second, me * width, width)
    branch = causal_conv(extended_next, weights_second, own_bias_next)

    branch_rows = scatter_rows(branch, slab_rows, chans)
    summed = (values + branch_rows).astype(jnp.bfloat16)
    return jnp.repeat(jnp.repeat(summed, 2, axis=1), 2, axis=2)


def solution(mesh):
    groups = mesh.shape["groups"]
    height = mesh.shape["height"]
    blocks = CHAN_BLOCKS
    split = Mesh(mesh.devices.reshape(groups, height // blocks, blocks), ("groups", "hz", "hq"))
    rows = ("groups", "hz", "hq")
    placed = (
        P(None, rows, None, None),
        P(),
        P(),
        P(None, ("hz", "hq"), None),
        P(),
        P(),
        P(),
        P(None, ("hz", "hq"), None),
        P(),
    )
    return jax.shard_map(
        per_device,
        mesh=split,
        in_specs=placed,
        out_specs=P(None, rows, None, None),
        check_vma=False,
    )
```

```python
import jax
import jax.numpy as jnp
from jax import lax
from jax.experimental import pallas as pl
from jax.experimental.pallas import tpu as pltpu
from jax.sharding import Mesh
from jax.sharding import PartitionSpec as P

GROUPS = 32
CHAN_BLOCKS = 4
EPS = 1e-06


def shift_pairs(count, step):
    return [(i, (i + step) % count) for i in range(count)]


def butterfly_stats(sums, squares, count, axes):
    for axis in axes:
        size = lax.axis_size(axis)
        bit = 1
        while bit < size:
            pairs = [(i, i ^ bit) for i in range(size)]
            other_sums, other_squares = lax.ppermute((sums, squares), axis, pairs)
            gap = sums - other_sums
            squares = (squares + other_squares) + gap * gap / (2.0 * count)
            sums = sums + other_sums
            count = count * 2
            bit *= 2
    return sums, squares, count


def local_stats(values, groups):
    frames, rows, cols, chans = values.shape
    grouped = values.reshape(frames * rows * cols, groups, chans // groups)
    count = float(frames * rows * cols * (chans // groups))
    sums = jnp.sum(grouped, axis=(0, 2))
    centred = grouped - (sums / count)[None, :, None]
    squares = jnp.sum(centred * centred, axis=(0, 2))
    return sums, squares, count


def group_scale(sums, squares, count, group_size):
    mean = sums / count
    scale = lax.rsqrt(squares / count + EPS)
    return jnp.repeat(mean, group_size), jnp.repeat(scale, group_size)


def activate(values, mean_chan, scale_chan, gain, shift):
    normed = (values - mean_chan) * scale_chan * gain + shift
    return jax.nn.silu(normed).astype(jnp.bfloat16)


def gather_blocks(block, axis_name, dim, total):
    size = lax.axis_size(axis_name)
    me = lax.axis_index(axis_name)
    width = block.shape[dim]
    shape = list(block.shape)
    shape[dim] = total
    out = jnp.zeros(shape, block.dtype)
    for step in range(size):
        piece = block if step == 0 else lax.ppermute(block, axis_name, shift_pairs(size, step))
        source = (me - step) % size
        start = [0] * len(shape)
        start[dim] = source * width
        out = lax.dynamic_update_slice(out, piece, start)
    return out


def with_row_halo(cells, axis_name):
    size = lax.axis_size(axis_name)
    down = [(i, i + 1) for i in range(size - 1)]
    up = [(i + 1, i) for i in range(size - 1)]
    top = lax.ppermute(cells[:, -1:], axis_name, down)
    bottom = lax.ppermute(cells[:, :1], axis_name, up)
    return jnp.concatenate([top, cells, bottom], axis=1)


def conv_body(x_ref, w_ref, b_ref, o_ref, acc_ref):
    step = pl.program_id(0)
    rows, cols, outs = o_ref.shape[1:]
    chans = x_ref.shape[-1]
    acc_ref[...] = jnp.broadcast_to(b_ref[...], acc_ref.shape)
    for i in range(3):
        for j in range(3):
            for k in range(3):
                patch = x_ref[step + i, pl.ds(j, rows), pl.ds(k, cols), :]
                acc_ref[...] += jnp.dot(
                    patch.reshape(rows * cols, chans),
                    w_ref[9 * i + 3 * j + k],
                    preferred_element_type=jnp.float32,
                )
    o_ref[0] = acc_ref[...].reshape(rows, cols, outs).astype(o_ref.dtype)


def causal_conv(extended, kernel, bias, out_dtype):
    leading = jnp.concatenate([extended[:1], extended[:1], extended], axis=0)
    padded = jnp.pad(leading, ((0, 0), (0, 0), (1, 1), (0, 0)))
    frames = extended.shape[0]
    rows = extended.shape[1] - 2
    cols = extended.shape[2]
    taps, chans, outs = kernel.shape
    flops = 2 * frames * rows * cols * chans * outs * taps
    moved = padded.size * 2 + kernel.size * 2 + frames * rows * cols * outs * 4
    return pl.pallas_call(
        conv_body,
        grid=(frames,),
        in_specs=[
            pl.BlockSpec(padded.shape, lambda t: (0, 0, 0, 0)),
            pl.BlockSpec(kernel.shape, lambda t: (0, 0, 0)),
            pl.BlockSpec((1, outs), lambda t: (0, 0)),
        ],
        out_specs=pl.BlockSpec((1, rows, cols, outs), lambda t: (t, 0, 0, 0)),
        out_shape=jax.ShapeDtypeStruct((frames, rows, cols, outs), out_dtype),
        scratch_shapes=[pltpu.VMEM((rows * cols, outs), jnp.float32)],
        cost_estimate=pl.CostEstimate(flops=flops, bytes_accessed=moved, transcendentals=0),
    )(padded, kernel, bias.reshape(1, outs))


def kernel_block(shard, chans):
    size = lax.axis_size("hq")
    me = lax.axis_index("hq")
    taps, in_block, outs = shard.shape
    width = outs // size
    out = jnp.zeros((taps, in_block * size, width), shard.dtype)
    for step in range(size):
        target = (me + step) % size
        piece = lax.dynamic_slice_in_dim(shard, target * width, width, axis=2)
        if step:
            piece = lax.ppermute(piece, "hq", shift_pairs(size, step))
        source = (me - step) % size
        out = lax.dynamic_update_slice(out, piece, (0, source * in_block, 0))
    return lax.all_gather(out, "hz", axis=1, tiled=True)


def scatter_rows(branch, slab_rows, chans):
    size = lax.axis_size("hq")
    me = lax.axis_index("hq")
    frames, rows, cols, width = branch.shape
    out = jnp.zeros((frames, slab_rows, cols, chans), branch.dtype)
    for step in range(size):
        target = (me + step) % size
        piece = lax.dynamic_slice_in_dim(branch, target * slab_rows, slab_rows, axis=1)
        if step:
            piece = lax.ppermute(piece, "hq", shift_pairs(size, step))
        source = (me - step) % size
        out = lax.dynamic_update_slice(out, piece, (0, 0, 0, source * width))
    return out


def per_device(
    latent,
    gain_first,
    shift_first,
    kernel_first,
    bias_first,
    gain_second,
    shift_second,
    kernel_second,
    bias_second,
):
    frames, slab_rows, cols, chans = latent.shape
    blocks = lax.axis_size("hq")
    width = chans // blocks
    me = lax.axis_index("hq")
    group_size = chans // GROUPS

    weights_first = kernel_block(kernel_first, chans)
    weights_second = kernel_block(kernel_second, chans)

    values = latent.astype(jnp.float32)
    sums, squares, count = local_stats(values, GROUPS)
    sums, squares, count = butterfly_stats(sums, squares, count, ("hq", "hz"))
    mean_chan, scale_chan = group_scale(sums, squares, count, group_size)
    act_first = activate(values, mean_chan, scale_chan, gain_first, shift_first)

    group_rows = gather_blocks(act_first, "hq", 1, slab_rows * blocks)
    extended = with_row_halo(group_rows, "hz")
    own_bias = lax.dynamic_slice_in_dim(bias_first, me * width, width)
    hidden = causal_conv(extended, weights_first, own_bias, jnp.bfloat16)

    hidden_values = hidden.astype(jnp.float32)
    sums, squares, count = local_stats(hidden_values, width // group_size)
    sums, squares, count = butterfly_stats(sums, squares, count, ("hz",))
    mean_own, scale_own = group_scale(sums, squares, count, group_size)
    own_gain = lax.dynamic_slice_in_dim(gain_second, me * width, width)
    own_shift = lax.dynamic_slice_in_dim(shift_second, me * width, width)
    act_second = activate(hidden_values, mean_own, scale_own, own_gain, own_shift)

    extended_next = with_row_halo(act_second, "hz")
    extended_next = gather_blocks(extended_next, "hq", 3, chans)
    own_bias_next = lax.dynamic_slice_in_dim(bias_second, me * width, width)
    branch = causal_conv(extended_next, weights_second, own_bias_next, jnp.float32)

    branch_rows = scatter_rows(branch, slab_rows, chans)
    summed = (values + branch_rows).astype(jnp.bfloat16)
    return jnp.repeat(jnp.repeat(summed, 2, axis=1), 2, axis=2)


def solution(mesh):
    groups = mesh.shape["groups"]
    height = mesh.shape["height"]
    blocks = CHAN_BLOCKS
    split = Mesh(mesh.devices.reshape(groups, height // blocks, blocks), ("groups", "hz", "hq"))
    rows = ("groups", "hz", "hq")
    placed = (
        P(None, rows, None, None),
        P(),
        P(),
        P(None, ("hz", "hq"), None),
        P(),
        P(),
        P(),
        P(None, ("hz", "hq"), None),
        P(),
    )
    return jax.shard_map(
        per_device,
        mesh=split,
        in_specs=placed,
        out_specs=P(None, rows, None, None),
        check_vma=False,
    )
```

```python
import jax
import jax.numpy as jnp
from jax import lax
from jax.experimental import pallas as pl
from jax.experimental.pallas import tpu as pltpu
from jax.sharding import Mesh
from jax.sharding import PartitionSpec as P

GROUPS = 32
CHAN_BLOCKS = 4
EPS = 1e-06
HQ = ("ha", "hb")


def shift_pairs(count, step):
    return [(i, (i + step) % count) for i in range(count)]


def butterfly_stats(sums, squares, count, axes):
    for axis in axes:
        size = lax.axis_size(axis)
        bit = 1
        while bit < size:
            pairs = [(i, i ^ bit) for i in range(size)]
            other_sums, other_squares = lax.ppermute((sums, squares), axis, pairs)
            gap = sums - other_sums
            squares = (squares + other_squares) + gap * gap / (2.0 * count)
            sums = sums + other_sums
            count = count * 2
            bit *= 2
    return sums, squares, count


def local_stats(values, groups):
    frames, rows, cols, chans = values.shape
    grouped = values.reshape(frames * rows * cols, groups, chans // groups)
    count = float(frames * rows * cols * (chans // groups))
    sums = jnp.sum(grouped, axis=(0, 2))
    centred = grouped - (sums / count)[None, :, None]
    squares = jnp.sum(centred * centred, axis=(0, 2))
    return sums, squares, count


def group_scale(sums, squares, count, group_size):
    mean = sums / count
    scale = lax.rsqrt(squares / count + EPS)
    return jnp.repeat(mean, group_size), jnp.repeat(scale, group_size)


def activate(values, mean_chan, scale_chan, gain, shift):
    normed = (values - mean_chan) * scale_chan * gain + shift
    return jax.nn.silu(normed).astype(jnp.bfloat16)


def chip_gather(block, dim):
    count_a = lax.axis_size("ha")
    count_b = lax.axis_size("hb")
    me_a = lax.axis_index("ha")
    me_b = lax.axis_index("hb")
    width = block.shape[dim]
    shape = list(block.shape)
    shape[dim] = width * count_a * count_b
    firsts = [block]
    sources = [me_a]
    for step in range(1, count_a):
        firsts.append(lax.ppermute(block, "ha", shift_pairs(count_a, step)))
        sources.append((me_a - step) % count_a)
    firsts = tuple(firsts)
    out = jnp.zeros(shape, block.dtype)
    for step in range(count_b):
        bundle = firsts if step == 0 else lax.ppermute(firsts, "hb", shift_pairs(count_b, step))
        source_b = (me_b - step) % count_b
        for piece, source_a in zip(bundle, sources):
            start = [0] * len(shape)
            start[dim] = (source_a * count_b + source_b) * width
            out = lax.dynamic_update_slice(out, piece, start)
    return out


def edge_mask(cells):
    size = lax.axis_size("hz")
    me = lax.axis_index("hz")
    rows = cells.shape[1]
    row = lax.broadcasted_iota(jnp.int32, (1, rows, 1, 1), 1)
    keep = ((row > 0) | (me > 0)) & ((row < rows - 1) | (me < size - 1))
    return jnp.where(keep, cells, jnp.zeros_like(cells))


def with_row_halo(cells, axis_name):
    size = lax.axis_size(axis_name)
    down = [(i, i + 1) for i in range(size - 1)]
    up = [(i + 1, i) for i in range(size - 1)]
    top = lax.ppermute(cells[:, -1:], axis_name, down)
    bottom = lax.ppermute(cells[:, :1], axis_name, up)
    return jnp.concatenate([top, cells, bottom], axis=1)


def conv_body(x_ref, w_ref, b_ref, o_ref, acc_ref):
    step = pl.program_id(0)
    rows, cols, outs = o_ref.shape[1:]
    chans = x_ref.shape[-1]
    acc_ref[...] = jnp.broadcast_to(b_ref[...], acc_ref.shape)
    for i in range(3):
        for j in range(3):
            for k in range(3):
                patch = x_ref[step + i, pl.ds(j, rows), pl.ds(k, cols), :]
                acc_ref[...] += jnp.dot(
                    patch.reshape(rows * cols, chans),
                    w_ref[9 * i + 3 * j + k],
                    preferred_element_type=jnp.float32,
                )
    o_ref[0] = acc_ref[...].reshape(rows, cols, outs).astype(o_ref.dtype)


def causal_conv(extended, kernel, bias, out_dtype):
    leading = jnp.concatenate([extended[:1], extended[:1], extended], axis=0)
    padded = jnp.pad(leading, ((0, 0), (0, 0), (1, 1), (0, 0)))
    frames = extended.shape[0]
    rows = extended.shape[1] - 2
    cols = extended.shape[2]
    taps, chans, outs = kernel.shape
    flops = 2 * frames * rows * cols * chans * outs * taps
    moved = padded.size * 2 + kernel.size * 2 + frames * rows * cols * outs * 4
    return pl.pallas_call(
        conv_body,
        grid=(frames,),
        in_specs=[
            pl.BlockSpec(padded.shape, lambda t: (0, 0, 0, 0)),
            pl.BlockSpec(kernel.shape, lambda t: (0, 0, 0)),
            pl.BlockSpec((1, outs), lambda t: (0, 0)),
        ],
        out_specs=pl.BlockSpec((1, rows, cols, outs), lambda t: (t, 0, 0, 0)),
        out_shape=jax.ShapeDtypeStruct((frames, rows, cols, outs), out_dtype),
        scratch_shapes=[pltpu.VMEM((rows * cols, outs), jnp.float32)],
        cost_estimate=pl.CostEstimate(flops=flops, bytes_accessed=moved, transcendentals=0),
    )(padded, kernel, bias.reshape(1, outs))


def kernel_block(shard, chans):
    size = lax.axis_size("ha") * lax.axis_size("hb")
    me = lax.axis_index(HQ)
    taps, in_block, outs = shard.shape
    width = outs // size
    out = jnp.zeros((taps, in_block * size, width), shard.dtype)
    for step in range(size):
        target = (me + step) % size
        piece = lax.dynamic_slice_in_dim(shard, target * width, width, axis=2)
        if step:
            piece = lax.ppermute(piece, HQ, shift_pairs(size, step))
        source = (me - step) % size
        out = lax.dynamic_update_slice(out, piece, (0, source * in_block, 0))
    return lax.all_gather(out, "hz", axis=1, tiled=True)


def scatter_rows(branch, slab_rows, chans):
    size = lax.axis_size("ha") * lax.axis_size("hb")
    me = lax.axis_index(HQ)
    frames, rows, cols, width = branch.shape
    out = jnp.zeros((frames, slab_rows, cols, chans), branch.dtype)
    for step in range(size):
        target = (me + step) % size
        piece = lax.dynamic_slice_in_dim(branch, target * slab_rows, slab_rows, axis=1)
        if step:
            piece = lax.ppermute(piece, HQ, shift_pairs(size, step))
        source = (me - step) % size
        out = lax.dynamic_update_slice(out, piece, (0, 0, 0, source * width))
    return out


def per_device(
    latent,
    gain_first,
    shift_first,
    kernel_first,
    bias_first,
    gain_second,
    shift_second,
    kernel_second,
    bias_second,
):
    frames, slab_rows, cols, chans = latent.shape
    blocks = lax.axis_size("ha") * lax.axis_size("hb")
    width = chans // blocks
    me = lax.axis_index(HQ)
    group_size = chans // GROUPS

    weights_first = kernel_block(kernel_first, chans)
    weights_second = kernel_block(kernel_second, chans)

    values = latent.astype(jnp.float32)
    sums, squares, count = local_stats(values, GROUPS)
    raw_rows = with_row_halo(chip_gather(latent, 1), "hz")
    sums, squares, count = butterfly_stats(sums, squares, count, ("ha", "hb", "hz"))
    mean_chan, scale_chan = group_scale(sums, squares, count, group_size)
    act_first = activate(raw_rows.astype(jnp.float32), mean_chan, scale_chan, gain_first, shift_first)
    own_bias = lax.dynamic_slice_in_dim(bias_first, me * width, width)
    hidden = causal_conv(edge_mask(act_first), weights_first, own_bias, jnp.bfloat16)

    sums, squares, count = local_stats(hidden.astype(jnp.float32), width // group_size)
    raw_next = chip_gather(with_row_halo(hidden, "hz"), 3)
    sums, squares, count = butterfly_stats(sums, squares, count, ("hz",))
    packed = chip_gather(jnp.stack([sums, squares]), 1)
    mean_chan, scale_chan = group_scale(packed[0], packed[1], count, group_size)
    act_second = activate(raw_next.astype(jnp.float32), mean_chan, scale_chan, gain_second, shift_second)
    own_bias_next = lax.dynamic_slice_in_dim(bias_second, me * width, width)
    branch = causal_conv(edge_mask(act_second), weights_second, own_bias_next, jnp.float32)

    branch_rows = scatter_rows(branch, slab_rows, chans)
    summed = (values + branch_rows).astype(jnp.bfloat16)
    return jnp.repeat(jnp.repeat(summed, 2, axis=1), 2, axis=2)


def solution(mesh):
    groups = mesh.shape["groups"]
    height = mesh.shape["height"]
    blocks = CHAN_BLOCKS
    split = Mesh(
        mesh.devices.reshape(groups, height // blocks, 2, blocks // 2),
        ("groups", "hz", "ha", "hb"),
    )
    rows = ("groups", "hz", "ha", "hb")
    slabs = ("hz", "ha", "hb")
    placed = (
        P(None, rows, None, None),
        P(),
        P(),
        P(None, slabs, None),
        P(),
        P(),
        P(),
        P(None, slabs, None),
        P(),
    )
    return jax.shard_map(
        per_device,
        mesh=split,
        in_specs=placed,
        out_specs=P(None, rows, None, None),
        check_vma=False,
    )
```

```python
import jax
import jax.numpy as jnp
from jax import lax
from jax.experimental import pallas as pl
from jax.experimental.pallas import tpu as pltpu
from jax.sharding import Mesh
from jax.sharding import PartitionSpec as P

GROUPS = 32
CHAN_BLOCKS = 4
EPS = 1e-06
HQ = ("ha", "hb")


def shift_pairs(count, step):
    return [(i, (i + step) % count) for i in range(count)]


def butterfly_stats(sums, squares, count, axes):
    for axis in axes:
        size = lax.axis_size(axis)
        bit = 1
        while bit < size:
            pairs = [(i, i ^ bit) for i in range(size)]
            other_sums, other_squares = lax.ppermute((sums, squares), axis, pairs)
            gap = sums - other_sums
            squares = (squares + other_squares) + gap * gap / (2.0 * count)
            sums = sums + other_sums
            count = count * 2
            bit *= 2
    return sums, squares, count


def local_stats(values, groups):
    frames, rows, cols, chans = values.shape
    grouped = values.reshape(frames * rows * cols, groups, chans // groups)
    count = float(frames * rows * cols * (chans // groups))
    sums = jnp.sum(grouped, axis=(0, 2))
    centred = grouped - (sums / count)[None, :, None]
    squares = jnp.sum(centred * centred, axis=(0, 2))
    return sums, squares, count


def group_scale(sums, squares, count, group_size):
    mean = sums / count
    scale = lax.rsqrt(squares / count + EPS)
    return jnp.repeat(mean, group_size), jnp.repeat(scale, group_size)


def activate(values, mean_chan, scale_chan, gain, shift):
    normed = (values - mean_chan) * scale_chan * gain + shift
    return jax.nn.silu(normed).astype(jnp.bfloat16)


def chip_gather(block, dim):
    count_a = lax.axis_size("ha")
    count_b = lax.axis_size("hb")
    me_a = lax.axis_index("ha")
    me_b = lax.axis_index("hb")
    width = block.shape[dim]
    shape = list(block.shape)
    shape[dim] = width * count_a * count_b
    firsts = [block]
    sources = [me_a]
    for step in range(1, count_a):
        firsts.append(lax.ppermute(block, "ha", shift_pairs(count_a, step)))
        sources.append((me_a - step) % count_a)
    firsts = tuple(firsts)
    out = jnp.zeros(shape, block.dtype)
    for step in range(count_b):
        bundle = firsts if step == 0 else lax.ppermute(firsts, "hb", shift_pairs(count_b, step))
        source_b = (me_b - step) % count_b
        for piece, source_a in zip(bundle, sources):
            start = [0] * len(shape)
            start[dim] = (source_a * count_b + source_b) * width
            out = lax.dynamic_update_slice(out, piece, start)
    return out


def edge_mask(cells):
    size = lax.axis_size("hz")
    me = lax.axis_index("hz")
    rows = cells.shape[1]
    row = lax.broadcasted_iota(jnp.int32, (1, rows, 1, 1), 1)
    keep = ((row > 0) | (me > 0)) & ((row < rows - 1) | (me < size - 1))
    return jnp.where(keep, cells, jnp.zeros_like(cells))


def with_row_halo(cells, axis_name):
    size = lax.axis_size(axis_name)
    down = [(i, i + 1) for i in range(size - 1)]
    up = [(i + 1, i) for i in range(size - 1)]
    top = lax.ppermute(cells[:, -1:], axis_name, down)
    bottom = lax.ppermute(cells[:, :1], axis_name, up)
    return jnp.concatenate([top, cells, bottom], axis=1)


def conv_body(x_ref, w_ref, b_ref, o_ref, acc_ref):
    step = pl.program_id(0)
    rows, cols, outs = o_ref.shape[1:]
    chans = x_ref.shape[-1]
    acc_ref[...] = jnp.broadcast_to(b_ref[...], acc_ref.shape)
    for i in range(3):
        for j in range(3):
            for k in range(3):
                patch = x_ref[step + i, pl.ds(j, rows), pl.ds(k, cols), :]
                acc_ref[...] += jnp.dot(
                    patch.reshape(rows * cols, chans),
                    w_ref[9 * i + 3 * j + k],
                    preferred_element_type=jnp.float32,
                )
    o_ref[0] = acc_ref[...].reshape(rows, cols, outs).astype(o_ref.dtype)


def causal_conv(extended, kernel, bias, out_dtype):
    leading = jnp.concatenate([extended[:1], extended[:1], extended], axis=0)
    padded = jnp.pad(leading, ((0, 0), (0, 0), (1, 1), (0, 0)))
    frames = extended.shape[0]
    rows = extended.shape[1] - 2
    cols = extended.shape[2]
    taps, chans, outs = kernel.shape
    flops = 2 * frames * rows * cols * chans * outs * taps
    moved = padded.size * 2 + kernel.size * 2 + frames * rows * cols * outs * 4
    return pl.pallas_call(
        conv_body,
        grid=(frames,),
        in_specs=[
            pl.BlockSpec(padded.shape, lambda t: (0, 0, 0, 0)),
            pl.BlockSpec(kernel.shape, lambda t: (0, 0, 0)),
            pl.BlockSpec((1, outs), lambda t: (0, 0)),
        ],
        out_specs=pl.BlockSpec((1, rows, cols, outs), lambda t: (t, 0, 0, 0)),
        out_shape=jax.ShapeDtypeStruct((frames, rows, cols, outs), out_dtype),
        scratch_shapes=[pltpu.VMEM((rows * cols, outs), jnp.float32)],
        cost_estimate=pl.CostEstimate(flops=flops, bytes_accessed=moved, transcendentals=0),
    )(padded, kernel, bias.reshape(1, outs))


def kernel_block(shard, chans):
    size = lax.axis_size("ha") * lax.axis_size("hb")
    me = lax.axis_index(HQ)
    taps, in_block, outs = shard.shape
    width = outs // size
    out = jnp.zeros((taps, in_block * size, width), shard.dtype)
    for step in range(size):
        target = (me + step) % size
        piece = lax.dynamic_slice_in_dim(shard, target * width, width, axis=2)
        if step:
            piece = lax.ppermute(piece, HQ, shift_pairs(size, step))
        source = (me - step) % size
        out = lax.dynamic_update_slice(out, piece, (0, source * in_block, 0))
    parts = lax.axis_size("groups")
    part = lax.axis_index("groups")
    share = width // parts
    mine = lax.dynamic_slice_in_dim(out, part * share, share, axis=2)
    gathered = lax.all_gather(mine, "hz", axis=1, tiled=True)
    result = jnp.zeros((taps, chans, width), shard.dtype)
    result = lax.dynamic_update_slice(result, gathered, (0, 0, part * share))
    for step in range(1, parts):
        other = lax.ppermute(gathered, "groups", shift_pairs(parts, step))
        source = (part - step) % parts
        result = lax.dynamic_update_slice(result, other, (0, 0, source * share))
    return result


def scatter_rows(branch, slab_rows, chans):
    size = lax.axis_size("ha") * lax.axis_size("hb")
    me = lax.axis_index(HQ)
    frames, rows, cols, width = branch.shape
    out = jnp.zeros((frames, slab_rows, cols, chans), branch.dtype)
    for step in range(size):
        target = (me + step) % size
        piece = lax.dynamic_slice_in_dim(branch, target * slab_rows, slab_rows, axis=1)
        if step:
            piece = lax.ppermute(piece, HQ, shift_pairs(size, step))
        source = (me - step) % size
        out = lax.dynamic_update_slice(out, piece, (0, 0, 0, source * width))
    return out


def per_device(
    latent,
    gain_first,
    shift_first,
    kernel_first,
    bias_first,
    gain_second,
    shift_second,
    kernel_second,
    bias_second,
):
    frames, slab_rows, cols, chans = latent.shape
    blocks = lax.axis_size("ha") * lax.axis_size("hb")
    width = chans // blocks
    me = lax.axis_index(HQ)
    group_size = chans // GROUPS

    weights_first = kernel_block(kernel_first, chans)
    weights_second = kernel_block(kernel_second, chans)

    values = latent.astype(jnp.float32)
    sums, squares, count = local_stats(values, GROUPS)
    raw_rows = with_row_halo(chip_gather(latent, 1), "hz")
    sums, squares, count = butterfly_stats(sums, squares, count, ("ha", "hb", "hz"))
    mean_chan, scale_chan = group_scale(sums, squares, count, group_size)
    act_first = activate(raw_rows.astype(jnp.float32), mean_chan, scale_chan, gain_first, shift_first)
    own_bias = lax.dynamic_slice_in_dim(bias_first, me * width, width)
    hidden = causal_conv(edge_mask(act_first), weights_first, own_bias, jnp.bfloat16)

    sums, squares, count = local_stats(hidden.astype(jnp.float32), width // group_size)
    raw_next = chip_gather(with_row_halo(hidden, "hz"), 3)
    sums, squares, count = butterfly_stats(sums, squares, count, ("hz",))
    packed = chip_gather(jnp.stack([sums, squares]), 1)
    mean_chan, scale_chan = group_scale(packed[0], packed[1], count, group_size)
    act_second = activate(raw_next.astype(jnp.float32), mean_chan, scale_chan, gain_second, shift_second)
    own_bias_next = lax.dynamic_slice_in_dim(bias_second, me * width, width)
    branch = causal_conv(edge_mask(act_second), weights_second, own_bias_next, jnp.float32)

    branch_rows = scatter_rows(branch, slab_rows, chans)
    summed = (values + branch_rows).astype(jnp.bfloat16)
    return jnp.repeat(jnp.repeat(summed, 2, axis=1), 2, axis=2)


def solution(mesh):
    groups = mesh.shape["groups"]
    height = mesh.shape["height"]
    blocks = CHAN_BLOCKS
    split = Mesh(
        mesh.devices.reshape(groups, height // blocks, 2, blocks // 2),
        ("groups", "hz", "ha", "hb"),
    )
    rows = ("groups", "hz", "ha", "hb")
    slabs = ("hz", "ha", "hb")
    placed = (
        P(None, rows, None, None),
        P(),
        P(),
        P(None, slabs, None),
        P(),
        P(),
        P(),
        P(None, slabs, None),
        P(),
    )
    return jax.shard_map(
        per_device,
        mesh=split,
        in_specs=placed,
        out_specs=P(None, rows, None, None),
        check_vma=False,
    )
```

```python
import jax
import jax.numpy as jnp
from jax import lax
from jax.experimental import pallas as pl
from jax.experimental.pallas import tpu as pltpu
from jax.sharding import Mesh
from jax.sharding import PartitionSpec as P

GROUPS = 32
CHAN_BLOCKS = 4
EPS = 1e-06
HQ = ("ha", "hb")


def shift_pairs(count, step):
    return [(i, (i + step) % count) for i in range(count)]


def butterfly_stats(sums, squares, count, axes):
    for axis in axes:
        size = lax.axis_size(axis)
        bit = 1
        while bit < size:
            pairs = [(i, i ^ bit) for i in range(size)]
            other_sums, other_squares = lax.ppermute((sums, squares), axis, pairs)
            gap = sums - other_sums
            squares = (squares + other_squares) + gap * gap / (2.0 * count)
            sums = sums + other_sums
            count = count * 2
            bit *= 2
    return sums, squares, count


def local_stats(values, groups):
    frames, rows, cols, chans = values.shape
    grouped = values.reshape(frames * rows * cols, groups, chans // groups)
    count = float(frames * rows * cols * (chans // groups))
    sums = jnp.sum(grouped, axis=(0, 2))
    centred = grouped - (sums / count)[None, :, None]
    squares = jnp.sum(centred * centred, axis=(0, 2))
    return sums, squares, count


def group_scale(sums, squares, count, group_size):
    mean = sums / count
    scale = lax.rsqrt(squares / count + EPS)
    return jnp.repeat(mean, group_size), jnp.repeat(scale, group_size)


def activate(values, mean_chan, scale_chan, gain, shift):
    normed = (values - mean_chan) * scale_chan * gain + shift
    return jax.nn.silu(normed).astype(jnp.bfloat16)


def chip_gather(block, dim):
    count_a = lax.axis_size("ha")
    count_b = lax.axis_size("hb")
    me_a = lax.axis_index("ha")
    me_b = lax.axis_index("hb")
    width = block.shape[dim]
    shape = list(block.shape)
    shape[dim] = width * count_a * count_b
    firsts = [block]
    sources = [me_a]
    for step in range(1, count_a):
        firsts.append(lax.ppermute(block, "ha", shift_pairs(count_a, step)))
        sources.append((me_a - step) % count_a)
    firsts = tuple(firsts)
    out = jnp.zeros(shape, block.dtype)
    for step in range(count_b):
        bundle = firsts if step == 0 else lax.ppermute(firsts, "hb", shift_pairs(count_b, step))
        source_b = (me_b - step) % count_b
        for piece, source_a in zip(bundle, sources):
            start = [0] * len(shape)
            start[dim] = (source_a * count_b + source_b) * width
            out = lax.dynamic_update_slice(out, piece, start)
    return out


def edge_mask(cells):
    size = lax.axis_size("hz")
    me = lax.axis_index("hz")
    rows = cells.shape[1]
    row = lax.broadcasted_iota(jnp.int32, (1, rows, 1, 1), 1)
    keep = ((row > 0) | (me > 0)) & ((row < rows - 1) | (me < size - 1))
    return jnp.where(keep, cells, jnp.zeros_like(cells))


def with_row_halo(cells, axis_name):
    size = lax.axis_size(axis_name)
    down = [(i, i + 1) for i in range(size - 1)]
    up = [(i + 1, i) for i in range(size - 1)]
    top = lax.ppermute(cells[:, -1:], axis_name, down)
    bottom = lax.ppermute(cells[:, :1], axis_name, up)
    return jnp.concatenate([top, cells, bottom], axis=1)


def conv_body(x_ref, w_ref, b_ref, o_ref, acc_ref):
    step = pl.program_id(0)
    rows, cols, outs = o_ref.shape[1:]
    chans = x_ref.shape[-1]
    acc_ref[...] = jnp.broadcast_to(b_ref[...], acc_ref.shape)
    for i in range(3):
        for j in range(3):
            for k in range(3):
                patch = x_ref[step + i, pl.ds(j, rows), pl.ds(k, cols), :]
                acc_ref[...] += jnp.dot(
                    patch.reshape(rows * cols, chans),
                    w_ref[9 * i + 3 * j + k],
                    preferred_element_type=jnp.float32,
                )
    o_ref[0] = acc_ref[...].reshape(rows, cols, outs).astype(o_ref.dtype)


def causal_conv(extended, kernel, bias, out_dtype):
    leading = jnp.concatenate([extended[:1], extended[:1], extended], axis=0)
    padded = jnp.pad(leading, ((0, 0), (0, 0), (1, 1), (0, 0)))
    frames = extended.shape[0]
    rows = extended.shape[1] - 2
    cols = extended.shape[2]
    taps, chans, outs = kernel.shape
    flops = 2 * frames * rows * cols * chans * outs * taps
    moved = padded.size * 2 + kernel.size * 2 + frames * rows * cols * outs * 4
    return pl.pallas_call(
        conv_body,
        grid=(frames,),
        in_specs=[
            pl.BlockSpec(padded.shape, lambda t: (0, 0, 0, 0)),
            pl.BlockSpec(kernel.shape, lambda t: (0, 0, 0)),
            pl.BlockSpec((1, outs), lambda t: (0, 0)),
        ],
        out_specs=pl.BlockSpec((1, rows, cols, outs), lambda t: (t, 0, 0, 0)),
        out_shape=jax.ShapeDtypeStruct((frames, rows, cols, outs), out_dtype),
        scratch_shapes=[pltpu.VMEM((rows * cols, outs), jnp.float32)],
        cost_estimate=pl.CostEstimate(flops=flops, bytes_accessed=moved, transcendentals=0),
    )(padded, kernel, bias.reshape(1, outs))


def kernel_block(shard, chans):
    size = lax.axis_size("ha") * lax.axis_size("hb")
    me = lax.axis_index(HQ)
    taps, in_block, outs = shard.shape
    width = outs // size
    flipped = jnp.transpose(shard, (1, 0, 2))
    out = jnp.zeros((in_block * size, taps, width), shard.dtype)
    for step in range(size):
        target = (me + step) % size
        piece = lax.dynamic_slice_in_dim(flipped, target * width, width, axis=2)
        if step:
            piece = lax.ppermute(piece, HQ, shift_pairs(size, step))
        source = (me - step) % size
        out = lax.dynamic_update_slice(out, piece, (source * in_block, 0, 0))
    parts = lax.axis_size("groups")
    part = lax.axis_index("groups")
    rows = lax.axis_size("hz")
    share = (in_block * size) // parts
    mine = lax.dynamic_slice_in_dim(out, part * share, share, axis=0)
    gathered = lax.all_gather(mine, "hz", axis=0)
    result = jnp.zeros((rows, parts, share, taps, width), shard.dtype)
    result = lax.dynamic_update_slice(result, gathered[:, None], (0, part, 0, 0, 0))
    for step in range(1, parts):
        other = lax.ppermute(gathered, "groups", shift_pairs(parts, step))
        source = (part - step) % parts
        result = lax.dynamic_update_slice(result, other[:, None], (0, source, 0, 0, 0))
    return jnp.transpose(result.reshape(chans, taps, width), (1, 0, 2))


def scatter_rows(branch, slab_rows, chans):
    size = lax.axis_size("ha") * lax.axis_size("hb")
    me = lax.axis_index(HQ)
    frames, rows, cols, width = branch.shape
    out = jnp.zeros((frames, slab_rows, cols, chans), branch.dtype)
    for step in range(size):
        target = (me + step) % size
        piece = lax.dynamic_slice_in_dim(branch, target * slab_rows, slab_rows, axis=1)
        if step:
            piece = lax.ppermute(piece, HQ, shift_pairs(size, step))
        source = (me - step) % size
        out = lax.dynamic_update_slice(out, piece, (0, 0, 0, source * width))
    return out


def per_device(
    latent,
    gain_first,
    shift_first,
    kernel_first,
    bias_first,
    gain_second,
    shift_second,
    kernel_second,
    bias_second,
):
    frames, slab_rows, cols, chans = latent.shape
    blocks = lax.axis_size("ha") * lax.axis_size("hb")
    width = chans // blocks
    me = lax.axis_index(HQ)
    group_size = chans // GROUPS

    weights_first = kernel_block(kernel_first, chans)
    weights_second = kernel_block(kernel_second, chans)

    values = latent.astype(jnp.float32)
    sums, squares, count = local_stats(values, GROUPS)
    raw_rows = with_row_halo(chip_gather(latent, 1), "hz")
    sums, squares, count = butterfly_stats(sums, squares, count, ("ha", "hb", "hz"))
    mean_chan, scale_chan = group_scale(sums, squares, count, group_size)
    act_first = activate(raw_rows.astype(jnp.float32), mean_chan, scale_chan, gain_first, shift_first)
    own_bias = lax.dynamic_slice_in_dim(bias_first, me * width, width)
    hidden = causal_conv(edge_mask(act_first), weights_first, own_bias, jnp.bfloat16)

    sums, squares, count = local_stats(hidden.astype(jnp.float32), width // group_size)
    raw_next = chip_gather(with_row_halo(hidden, "hz"), 3)
    sums, squares, count = butterfly_stats(sums, squares, count, ("hz",))
    packed = chip_gather(jnp.stack([sums, squares]), 1)
    mean_chan, scale_chan = group_scale(packed[0], packed[1], count, group_size)
    act_second = activate(raw_next.astype(jnp.float32), mean_chan, scale_chan, gain_second, shift_second)
    own_bias_next = lax.dynamic_slice_in_dim(bias_second, me * width, width)
    branch = causal_conv(edge_mask(act_second), weights_second, own_bias_next, jnp.float32)

    branch_rows = scatter_rows(branch, slab_rows, chans)
    summed = (values + branch_rows).astype(jnp.bfloat16)
    return jnp.repeat(jnp.repeat(summed, 2, axis=1), 2, axis=2)


def solution(mesh):
    groups = mesh.shape["groups"]
    height = mesh.shape["height"]
    blocks = CHAN_BLOCKS
    split = Mesh(
        mesh.devices.reshape(groups, height // blocks, 2, blocks // 2),
        ("groups", "hz", "ha", "hb"),
    )
    rows = ("groups", "hz", "ha", "hb")
    slabs = ("hz", "ha", "hb")
    placed = (
        P(None, rows, None, None),
        P(),
        P(),
        P(None, slabs, None),
        P(),
        P(),
        P(),
        P(None, slabs, None),
        P(),
    )
    return jax.shard_map(
        per_device,
        mesh=split,
        in_specs=placed,
        out_specs=P(None, rows, None, None),
        check_vma=False,
    )
```

```python
import jax
import jax.numpy as jnp
from jax import lax
from jax.experimental import pallas as pl
from jax.experimental.pallas import tpu as pltpu
from jax.sharding import Mesh
from jax.sharding import PartitionSpec as P

GROUPS = 32
CHAN_BLOCKS = 4
EPS = 1e-06
HQ = ("ha", "hb")


def shift_pairs(count, step):
    return [(i, (i + step) % count) for i in range(count)]


def butterfly_stats(sums, squares, count, axes):
    for axis in axes:
        size = lax.axis_size(axis)
        bit = 1
        while bit < size:
            pairs = [(i, i ^ bit) for i in range(size)]
            other_sums, other_squares = lax.ppermute((sums, squares), axis, pairs)
            gap = sums - other_sums
            squares = (squares + other_squares) + gap * gap / (2.0 * count)
            sums = sums + other_sums
            count = count * 2
            bit *= 2
    return sums, squares, count


def local_stats(values, groups):
    frames, rows, cols, chans = values.shape
    grouped = values.reshape(frames * rows * cols, groups, chans // groups)
    count = float(frames * rows * cols * (chans // groups))
    sums = jnp.sum(grouped, axis=(0, 2))
    centred = grouped - (sums / count)[None, :, None]
    squares = jnp.sum(centred * centred, axis=(0, 2))
    return sums, squares, count


def group_scale(sums, squares, count, group_size):
    mean = sums / count
    scale = lax.rsqrt(squares / count + EPS)
    return jnp.repeat(mean, group_size), jnp.repeat(scale, group_size)


def activate(values, mean_chan, scale_chan, gain, shift):
    normed = (values - mean_chan) * scale_chan * gain + shift
    return jax.nn.silu(normed).astype(jnp.bfloat16)


def chip_gather(block, dim):
    count_a = lax.axis_size("ha")
    count_b = lax.axis_size("hb")
    me_a = lax.axis_index("ha")
    me_b = lax.axis_index("hb")
    width = block.shape[dim]
    shape = list(block.shape)
    shape[dim] = width * count_a * count_b
    firsts = [block]
    sources = [me_a]
    for step in range(1, count_a):
        firsts.append(lax.ppermute(block, "ha", shift_pairs(count_a, step)))
        sources.append((me_a - step) % count_a)
    firsts = tuple(firsts)
    out = jnp.zeros(shape, block.dtype)
    for step in range(count_b):
        bundle = firsts if step == 0 else lax.ppermute(firsts, "hb", shift_pairs(count_b, step))
        source_b = (me_b - step) % count_b
        for piece, source_a in zip(bundle, sources):
            start = [0] * len(shape)
            start[dim] = (source_a * count_b + source_b) * width
            out = lax.dynamic_update_slice(out, piece, start)
    return out


def edge_mask(cells):
    size = lax.axis_size("hz")
    me = lax.axis_index("hz")
    rows = cells.shape[1]
    row = lax.broadcasted_iota(jnp.int32, (1, rows, 1, 1), 1)
    keep = ((row > 0) | (me > 0)) & ((row < rows - 1) | (me < size - 1))
    return jnp.where(keep, cells, jnp.zeros_like(cells))


def with_row_halo(cells, axis_name):
    size = lax.axis_size(axis_name)
    down = [(i, i + 1) for i in range(size - 1)]
    up = [(i + 1, i) for i in range(size - 1)]
    top = lax.ppermute(cells[:, -1:], axis_name, down)
    bottom = lax.ppermute(cells[:, :1], axis_name, up)
    return jnp.concatenate([top, cells, bottom], axis=1)


def conv_body(x_ref, w_ref, b_ref, o_ref, acc_ref):
    step = pl.program_id(0)
    rows, cols, outs = o_ref.shape[1:]
    chans = x_ref.shape[-1]
    acc_ref[...] = jnp.broadcast_to(b_ref[...], acc_ref.shape)
    for i in range(3):
        for j in range(3):
            for k in range(3):
                patch = x_ref[step + i, pl.ds(j, rows), pl.ds(k, cols), :]
                acc_ref[...] += jnp.dot(
                    patch.reshape(rows * cols, chans),
                    w_ref[9 * i + 3 * j + k],
                    preferred_element_type=jnp.float32,
                )
    o_ref[0] = acc_ref[...].reshape(rows, cols, outs).astype(o_ref.dtype)


def causal_conv(extended, kernel, bias, out_dtype):
    leading = jnp.concatenate([extended[:1], extended[:1], extended], axis=0)
    padded = jnp.pad(leading, ((0, 0), (0, 0), (1, 1), (0, 0)))
    frames = extended.shape[0]
    rows = extended.shape[1] - 2
    cols = extended.shape[2]
    taps, chans, outs = kernel.shape
    flops = 2 * frames * rows * cols * chans * outs * taps
    moved = padded.size * 2 + kernel.size * 2 + frames * rows * cols * outs * 4
    return pl.pallas_call(
        conv_body,
        grid=(frames,),
        in_specs=[
            pl.BlockSpec(padded.shape, lambda t: (0, 0, 0, 0)),
            pl.BlockSpec(kernel.shape, lambda t: (0, 0, 0)),
            pl.BlockSpec((1, outs), lambda t: (0, 0)),
        ],
        out_specs=pl.BlockSpec((1, rows, cols, outs), lambda t: (t, 0, 0, 0)),
        out_shape=jax.ShapeDtypeStruct((frames, rows, cols, outs), out_dtype),
        scratch_shapes=[pltpu.VMEM((rows * cols, outs), jnp.float32)],
        cost_estimate=pl.CostEstimate(flops=flops, bytes_accessed=moved, transcendentals=0),
    )(padded, kernel, bias.reshape(1, outs))


def kernel_block(shard, chans):
    size = lax.axis_size("ha") * lax.axis_size("hb")
    me = lax.axis_index(HQ)
    taps, in_block, outs = shard.shape
    width = outs // size
    flipped = jnp.transpose(shard, (1, 0, 2))
    out = jnp.zeros((in_block * size, taps, width), shard.dtype)
    for step in range(size):
        target = (me + step) % size
        piece = lax.dynamic_slice_in_dim(flipped, target * width, width, axis=2)
        if step:
            piece = lax.ppermute(piece, HQ, shift_pairs(size, step))
        source = (me - step) % size
        out = lax.dynamic_update_slice(out, piece, (source * in_block, 0, 0))
    parts = lax.axis_size("groups")
    share = (in_block * size) // parts
    part = lax.axis_index("groups")
    mine = lax.dynamic_slice_in_dim(out, part * share, share, axis=0)
    return lax.all_gather(mine, "hz", axis=0)


def swap_shares(gathered):
    parts = lax.axis_size("groups")
    part = lax.axis_index("groups")
    received = [gathered]
    for step in range(1, parts):
        received.append(lax.ppermute(gathered, "groups", shift_pairs(parts, step)))
    slots = []
    for slot in range(parts):
        piece = received[0]
        for step in range(1, parts):
            piece = jnp.where((part - step) % parts == slot, received[step], piece)
        slots.append(piece)
    rows, share, taps, width = gathered.shape
    stacked = jnp.stack(slots, axis=1).reshape(rows * parts * share, taps, width)
    return jnp.transpose(stacked, (1, 0, 2))


def scatter_rows(branch, slab_rows, chans):
    size = lax.axis_size("ha") * lax.axis_size("hb")
    me = lax.axis_index(HQ)
    frames, rows, cols, width = branch.shape
    out = jnp.zeros((frames, slab_rows, cols, chans), branch.dtype)
    for step in range(size):
        target = (me + step) % size
        piece = lax.dynamic_slice_in_dim(branch, target * slab_rows, slab_rows, axis=1)
        if step:
            piece = lax.ppermute(piece, HQ, shift_pairs(size, step))
        source = (me - step) % size
        out = lax.dynamic_update_slice(out, piece, (0, 0, 0, source * width))
    return out


def per_device(
    latent,
    gain_first,
    shift_first,
    kernel_first,
    bias_first,
    gain_second,
    shift_second,
    kernel_second,
    bias_second,
):
    frames, slab_rows, cols, chans = latent.shape
    blocks = lax.axis_size("ha") * lax.axis_size("hb")
    width = chans // blocks
    me = lax.axis_index(HQ)
    group_size = chans // GROUPS

    weights_first = swap_shares(kernel_block(kernel_first, chans))
    gathered_second = kernel_block(kernel_second, chans)

    values = latent.astype(jnp.float32)
    sums, squares, count = local_stats(values, GROUPS)
    raw_rows = with_row_halo(chip_gather(latent, 1), "hz")
    sums, squares, count = butterfly_stats(sums, squares, count, ("ha", "hb", "hz"))
    mean_chan, scale_chan = group_scale(sums, squares, count, group_size)
    act_first = activate(raw_rows.astype(jnp.float32), mean_chan, scale_chan, gain_first, shift_first)
    own_bias = lax.dynamic_slice_in_dim(bias_first, me * width, width)
    hidden = causal_conv(edge_mask(act_first), weights_first, own_bias, jnp.bfloat16)

    hidden, gathered_second = lax.optimization_barrier((hidden, gathered_second))
    weights_second = swap_shares(gathered_second)
    sums, squares, count = local_stats(hidden.astype(jnp.float32), width // group_size)
    raw_next = chip_gather(with_row_halo(hidden, "hz"), 3)
    sums, squares, count = butterfly_stats(sums, squares, count, ("hz",))
    packed = chip_gather(jnp.stack([sums, squares]), 1)
    mean_chan, scale_chan = group_scale(packed[0], packed[1], count, group_size)
    act_second = activate(raw_next.astype(jnp.float32), mean_chan, scale_chan, gain_second, shift_second)
    own_bias_next = lax.dynamic_slice_in_dim(bias_second, me * width, width)
    branch = causal_conv(edge_mask(act_second), weights_second, own_bias_next, jnp.float32)

    branch_rows = scatter_rows(branch, slab_rows, chans)
    summed = (values + branch_rows).astype(jnp.bfloat16)
    return jnp.repeat(jnp.repeat(summed, 2, axis=1), 2, axis=2)


def solution(mesh):
    groups = mesh.shape["groups"]
    height = mesh.shape["height"]
    blocks = CHAN_BLOCKS
    split = Mesh(
        mesh.devices.reshape(groups, height // blocks, 2, blocks // 2),
        ("groups", "hz", "ha", "hb"),
    )
    rows = ("groups", "hz", "ha", "hb")
    slabs = ("hz", "ha", "hb")
    placed = (
        P(None, rows, None, None),
        P(),
        P(),
        P(None, slabs, None),
        P(),
        P(),
        P(),
        P(None, slabs, None),
        P(),
    )
    return jax.shard_map(
        per_device,
        mesh=split,
        in_specs=placed,
        out_specs=P(None, rows, None, None),
        check_vma=False,
    )
```

```python
import jax
import jax.numpy as jnp
from jax import lax
from jax.experimental import pallas as pl
from jax.experimental.pallas import tpu as pltpu
from jax.sharding import Mesh
from jax.sharding import PartitionSpec as P

GROUPS = 32
CHAN_BLOCKS = 4
EPS = 1e-06
HQ = ("ha", "hb")


def shift_pairs(count, step):
    return [(i, (i + step) % count) for i in range(count)]


def butterfly_stats(sums, squares, count, axes):
    for axis in axes:
        size = lax.axis_size(axis)
        bit = 1
        while bit < size:
            pairs = [(i, i ^ bit) for i in range(size)]
            other_sums, other_squares = lax.ppermute((sums, squares), axis, pairs)
            gap = sums - other_sums
            squares = (squares + other_squares) + gap * gap / (2.0 * count)
            sums = sums + other_sums
            count = count * 2
            bit *= 2
    return sums, squares, count


def local_stats(values, groups):
    frames, rows, cols, chans = values.shape
    grouped = values.reshape(frames * rows * cols, groups, chans // groups)
    count = float(frames * rows * cols * (chans // groups))
    sums = jnp.sum(grouped, axis=(0, 2))
    centred = grouped - (sums / count)[None, :, None]
    squares = jnp.sum(centred * centred, axis=(0, 2))
    return sums, squares, count


def group_scale(sums, squares, count, group_size):
    mean = sums / count
    scale = lax.rsqrt(squares / count + EPS)
    return jnp.repeat(mean, group_size), jnp.repeat(scale, group_size)


def activate(values, mean_chan, scale_chan, gain, shift):
    normed = (values - mean_chan) * scale_chan * gain + shift
    return jax.nn.silu(normed).astype(jnp.bfloat16)


def chip_gather(block, dim):
    count_a = lax.axis_size("ha")
    count_b = lax.axis_size("hb")
    me_a = lax.axis_index("ha")
    me_b = lax.axis_index("hb")
    width = block.shape[dim]
    shape = list(block.shape)
    shape[dim] = width * count_a * count_b
    firsts = [block]
    sources = [me_a]
    for step in range(1, count_a):
        firsts.append(lax.ppermute(block, "ha", shift_pairs(count_a, step)))
        sources.append((me_a - step) % count_a)
    firsts = tuple(firsts)
    out = jnp.zeros(shape, block.dtype)
    for step in range(count_b):
        bundle = firsts if step == 0 else lax.ppermute(firsts, "hb", shift_pairs(count_b, step))
        source_b = (me_b - step) % count_b
        for piece, source_a in zip(bundle, sources):
            start = [0] * len(shape)
            start[dim] = (source_a * count_b + source_b) * width
            out = lax.dynamic_update_slice(out, piece, start)
    return out


def edge_mask(cells):
    size = lax.axis_size("hz")
    me = lax.axis_index("hz")
    rows = cells.shape[1]
    row = lax.broadcasted_iota(jnp.int32, (1, rows, 1, 1), 1)
    keep = ((row > 0) | (me > 0)) & ((row < rows - 1) | (me < size - 1))
    return jnp.where(keep, cells, jnp.zeros_like(cells))


def with_row_halo(cells, axis_name):
    size = lax.axis_size(axis_name)
    down = [(i, i + 1) for i in range(size - 1)]
    up = [(i + 1, i) for i in range(size - 1)]
    top = lax.ppermute(cells[:, -1:], axis_name, down)
    bottom = lax.ppermute(cells[:, :1], axis_name, up)
    return jnp.concatenate([top, cells, bottom], axis=1)


def conv_body(x_ref, w_ref, b_ref, o_ref, acc_ref):
    step = pl.program_id(0)
    rows, cols, outs = o_ref.shape[1:]
    chans = x_ref.shape[-1]
    acc_ref[...] = jnp.broadcast_to(b_ref[...], acc_ref.shape)
    for i in range(3):
        for j in range(3):
            for k in range(3):
                patch = x_ref[step + i, pl.ds(j, rows), pl.ds(k, cols), :]
                acc_ref[...] += jnp.dot(
                    patch.reshape(rows * cols, chans),
                    w_ref[9 * i + 3 * j + k],
                    preferred_element_type=jnp.float32,
                )
    o_ref[0] = acc_ref[...].reshape(rows, cols, outs).astype(o_ref.dtype)


def causal_conv(extended, kernel, bias, out_dtype):
    leading = jnp.concatenate([extended[:1], extended[:1], extended], axis=0)
    padded = jnp.pad(leading, ((0, 0), (0, 0), (1, 1), (0, 0)))
    frames = extended.shape[0]
    rows = extended.shape[1] - 2
    cols = extended.shape[2]
    taps, chans, outs = kernel.shape
    flops = 2 * frames * rows * cols * chans * outs * taps
    moved = padded.size * 2 + kernel.size * 2 + frames * rows * cols * outs * 4
    return pl.pallas_call(
        conv_body,
        grid=(frames,),
        in_specs=[
            pl.BlockSpec(padded.shape, lambda t: (0, 0, 0, 0)),
            pl.BlockSpec(kernel.shape, lambda t: (0, 0, 0)),
            pl.BlockSpec((1, outs), lambda t: (0, 0)),
        ],
        out_specs=pl.BlockSpec((1, rows, cols, outs), lambda t: (t, 0, 0, 0)),
        out_shape=jax.ShapeDtypeStruct((frames, rows, cols, outs), out_dtype),
        scratch_shapes=[pltpu.VMEM((rows * cols, outs), jnp.float32)],
        cost_estimate=pl.CostEstimate(flops=flops, bytes_accessed=moved, transcendentals=0),
    )(padded, kernel, bias.reshape(1, outs))


def kernel_block(shard, chans):
    size = lax.axis_size("ha") * lax.axis_size("hb")
    me = lax.axis_index(HQ)
    taps, in_block, outs = shard.shape
    width = outs // size
    out = jnp.zeros((taps, in_block * size, width), shard.dtype)
    for step in range(size):
        target = (me + step) % size
        piece = lax.dynamic_slice_in_dim(shard, target * width, width, axis=2)
        if step:
            piece = lax.ppermute(piece, HQ, shift_pairs(size, step))
        source = (me - step) % size
        out = lax.dynamic_update_slice(out, piece, (0, source * in_block, 0))
    parts = lax.axis_size("groups")
    part = lax.axis_index("groups")
    rows = lax.axis_size("hz")
    share = (in_block * size) // parts
    mine = lax.dynamic_slice_in_dim(out, part * share, share, axis=1)
    gathered = lax.all_gather(mine, ("groups", "hz"), axis=1, tiled=True)
    ordered = gathered.reshape(taps, parts, rows, share, width)
    return jnp.transpose(ordered, (0, 2, 1, 3, 4)).reshape(taps, chans, width)


def scatter_rows(branch, slab_rows, chans):
    size = lax.axis_size("ha") * lax.axis_size("hb")
    me = lax.axis_index(HQ)
    frames, rows, cols, width = branch.shape
    out = jnp.zeros((frames, slab_rows, cols, chans), branch.dtype)
    for step in range(size):
        target = (me + step) % size
        piece = lax.dynamic_slice_in_dim(branch, target * slab_rows, slab_rows, axis=1)
        if step:
            piece = lax.ppermute(piece, HQ, shift_pairs(size, step))
        source = (me - step) % size
        out = lax.dynamic_update_slice(out, piece, (0, 0, 0, source * width))
    return out


def per_device(
    latent,
    gain_first,
    shift_first,
    kernel_first,
    bias_first,
    gain_second,
    shift_second,
    kernel_second,
    bias_second,
):
    frames, slab_rows, cols, chans = latent.shape
    blocks = lax.axis_size("ha") * lax.axis_size("hb")
    width = chans // blocks
    me = lax.axis_index(HQ)
    group_size = chans // GROUPS

    weights_first = kernel_block(kernel_first, chans)
    weights_second = kernel_block(kernel_second, chans)

    values = latent.astype(jnp.float32)
    sums, squares, count = local_stats(values, GROUPS)
    raw_rows = with_row_halo(chip_gather(latent, 1), "hz")
    sums, squares, count = butterfly_stats(sums, squares, count, ("ha", "hb", "hz"))
    mean_chan, scale_chan = group_scale(sums, squares, count, group_size)
    act_first = activate(raw_rows.astype(jnp.float32), mean_chan, scale_chan, gain_first, shift_first)
    own_bias = lax.dynamic_slice_in_dim(bias_first, me * width, width)
    hidden = causal_conv(edge_mask(act_first), weights_first, own_bias, jnp.bfloat16)

    sums, squares, count = local_stats(hidden.astype(jnp.float32), width // group_size)
    raw_next = chip_gather(with_row_halo(hidden, "hz"), 3)
    sums, squares, count = butterfly_stats(sums, squares, count, ("hz",))
    packed = chip_gather(jnp.stack([sums, squares]), 1)
    mean_chan, scale_chan = group_scale(packed[0], packed[1], count, group_size)
    act_second = activate(raw_next.astype(jnp.float32), mean_chan, scale_chan, gain_second, shift_second)
    own_bias_next = lax.dynamic_slice_in_dim(bias_second, me * width, width)
    branch = causal_conv(edge_mask(act_second), weights_second, own_bias_next, jnp.float32)

    own_latent = lax.dynamic_slice_in_dim(raw_rows[:, 1:-1], me * width, width, axis=3)
    summed = (own_latent.astype(jnp.float32) + branch).astype(jnp.bfloat16)
    summed_rows = scatter_rows(summed, slab_rows, chans)
    return jnp.repeat(jnp.repeat(summed_rows, 2, axis=1), 2, axis=2)


def solution(mesh):
    groups = mesh.shape["groups"]
    height = mesh.shape["height"]
    blocks = CHAN_BLOCKS
    split = Mesh(
        mesh.devices.reshape(groups, height // blocks, 2, blocks // 2),
        ("groups", "hz", "ha", "hb"),
    )
    rows = ("groups", "hz", "ha", "hb")
    slabs = ("hz", "ha", "hb")
    placed = (
        P(None, rows, None, None),
        P(),
        P(),
        P(None, slabs, None),
        P(),
        P(),
        P(),
        P(None, slabs, None),
        P(),
    )
    return jax.shard_map(
        per_device,
        mesh=split,
        in_specs=placed,
        out_specs=P(None, rows, None, None),
        check_vma=False,
    )
```

```python
import jax
import jax.numpy as jnp
from jax import lax
from jax.experimental import pallas as pl
from jax.experimental.pallas import tpu as pltpu
from jax.sharding import Mesh
from jax.sharding import PartitionSpec as P

GROUPS = 32
CHAN_BLOCKS = 4
EPS = 1e-06
HQ = ("ha", "hb")


def shift_pairs(count, step):
    return [(i, (i + step) % count) for i in range(count)]


def butterfly_stats(sums, squares, count, axes):
    for axis in axes:
        size = lax.axis_size(axis)
        bit = 1
        while bit < size:
            pairs = [(i, i ^ bit) for i in range(size)]
            other_sums, other_squares = lax.ppermute((sums, squares), axis, pairs)
            gap = sums - other_sums
            squares = (squares + other_squares) + gap * gap / (2.0 * count)
            sums = sums + other_sums
            count = count * 2
            bit *= 2
    return sums, squares, count


def local_stats(values, groups):
    frames, rows, cols, chans = values.shape
    grouped = values.reshape(frames * rows * cols, groups, chans // groups)
    count = float(frames * rows * cols * (chans // groups))
    sums = jnp.sum(grouped, axis=(0, 2))
    centred = grouped - (sums / count)[None, :, None]
    squares = jnp.sum(centred * centred, axis=(0, 2))
    return sums, squares, count


def group_scale(sums, squares, count, group_size):
    mean = sums / count
    scale = lax.rsqrt(squares / count + EPS)
    return jnp.repeat(mean, group_size), jnp.repeat(scale, group_size)


def activate(values, mean_chan, scale_chan, gain, shift):
    normed = (values - mean_chan) * scale_chan * gain + shift
    return jax.nn.silu(normed).astype(jnp.bfloat16)


def chip_gather(block, dim):
    count_a = lax.axis_size("ha")
    count_b = lax.axis_size("hb")
    me_a = lax.axis_index("ha")
    me_b = lax.axis_index("hb")
    width = block.shape[dim]
    shape = list(block.shape)
    shape[dim] = width * count_a * count_b
    firsts = [block]
    sources = [me_a]
    for step in range(1, count_a):
        firsts.append(lax.ppermute(block, "ha", shift_pairs(count_a, step)))
        sources.append((me_a - step) % count_a)
    firsts = tuple(firsts)
    out = jnp.zeros(shape, block.dtype)
    for step in range(count_b):
        bundle = firsts if step == 0 else lax.ppermute(firsts, "hb", shift_pairs(count_b, step))
        source_b = (me_b - step) % count_b
        for piece, source_a in zip(bundle, sources):
            start = [0] * len(shape)
            start[dim] = (source_a * count_b + source_b) * width
            out = lax.dynamic_update_slice(out, piece, start)
    return out


def edge_mask(cells):
    size = lax.axis_size("hz")
    me = lax.axis_index("hz")
    rows = cells.shape[1]
    row = lax.broadcasted_iota(jnp.int32, (1, rows, 1, 1), 1)
    keep = ((row > 0) | (me > 0)) & ((row < rows - 1) | (me < size - 1))
    return jnp.where(keep, cells, jnp.zeros_like(cells))


def with_row_halo(cells, axis_name):
    size = lax.axis_size(axis_name)
    down = [(i, i + 1) for i in range(size - 1)]
    up = [(i + 1, i) for i in range(size - 1)]
    top = lax.ppermute(cells[:, -1:], axis_name, down)
    bottom = lax.ppermute(cells[:, :1], axis_name, up)
    return jnp.concatenate([top, cells, bottom], axis=1)


def conv_body(x_ref, w_ref, b_ref, o_ref, acc_ref):
    step = pl.program_id(0)
    rows, cols, outs = o_ref.shape[1:]
    chans = x_ref.shape[-1]
    acc_ref[...] = jnp.broadcast_to(b_ref[...], acc_ref.shape)
    for i in range(3):
        for j in range(3):
            for k in range(3):
                patch = x_ref[step + i, pl.ds(j, rows), pl.ds(k, cols), :]
                acc_ref[...] += jnp.dot(
                    patch.reshape(rows * cols, chans),
                    w_ref[9 * i + 3 * j + k],
                    preferred_element_type=jnp.float32,
                )
    o_ref[0] = acc_ref[...].reshape(rows, cols, outs).astype(o_ref.dtype)


def causal_conv(extended, kernel, bias, out_dtype):
    leading = jnp.concatenate([extended[:1], extended[:1], extended], axis=0)
    padded = jnp.pad(leading, ((0, 0), (0, 0), (1, 1), (0, 0)))
    frames = extended.shape[0]
    rows = extended.shape[1] - 2
    cols = extended.shape[2]
    taps, chans, outs = kernel.shape
    flops = 2 * frames * rows * cols * chans * outs * taps
    moved = padded.size * 2 + kernel.size * 2 + frames * rows * cols * outs * 4
    return pl.pallas_call(
        conv_body,
        grid=(frames,),
        in_specs=[
            pl.BlockSpec(padded.shape, lambda t: (0, 0, 0, 0)),
            pl.BlockSpec(kernel.shape, lambda t: (0, 0, 0)),
            pl.BlockSpec((1, outs), lambda t: (0, 0)),
        ],
        out_specs=pl.BlockSpec((1, rows, cols, outs), lambda t: (t, 0, 0, 0)),
        out_shape=jax.ShapeDtypeStruct((frames, rows, cols, outs), out_dtype),
        scratch_shapes=[pltpu.VMEM((rows * cols, outs), jnp.float32)],
        cost_estimate=pl.CostEstimate(flops=flops, bytes_accessed=moved, transcendentals=0),
    )(padded, kernel, bias.reshape(1, outs))


def kernel_block(shard, chans):
    size = lax.axis_size("ha") * lax.axis_size("hb")
    taps, in_block, outs = shard.shape
    width = outs // size
    pieces = jnp.transpose(shard.reshape(taps, in_block, size, width), (2, 0, 1, 3))
    pieces = lax.all_to_all(pieces, HQ, 0, 0, tiled=True)
    out = jnp.transpose(pieces, (1, 0, 2, 3)).reshape(taps, size * in_block, width)
    return lax.all_gather(out, "hz", axis=1, tiled=True)


def scatter_rows(branch, slab_rows, chans):
    size = lax.axis_size("ha") * lax.axis_size("hb")
    me = lax.axis_index(HQ)
    frames, rows, cols, width = branch.shape
    out = jnp.zeros((frames, slab_rows, cols, chans), branch.dtype)
    for step in range(size):
        target = (me + step) % size
        piece = lax.dynamic_slice_in_dim(branch, target * slab_rows, slab_rows, axis=1)
        if step:
            piece = lax.ppermute(piece, HQ, shift_pairs(size, step))
        source = (me - step) % size
        out = lax.dynamic_update_slice(out, piece, (0, 0, 0, source * width))
    return out


def per_device(
    latent,
    gain_first,
    shift_first,
    kernel_first,
    bias_first,
    gain_second,
    shift_second,
    kernel_second,
    bias_second,
):
    frames, slab_rows, cols, chans = latent.shape
    blocks = lax.axis_size("ha") * lax.axis_size("hb")
    width = chans // blocks
    me = lax.axis_index(HQ)
    group_size = chans // GROUPS

    weights_first = kernel_block(kernel_first, chans)
    weights_second = kernel_block(kernel_second, chans)

    values = latent.astype(jnp.float32)
    sums, squares, count = local_stats(values, GROUPS)
    raw_rows = with_row_halo(chip_gather(latent, 1), "hz")
    sums, squares, count = butterfly_stats(sums, squares, count, ("ha", "hb", "hz"))
    mean_chan, scale_chan = group_scale(sums, squares, count, group_size)
    act_first = activate(raw_rows.astype(jnp.float32), mean_chan, scale_chan, gain_first, shift_first)
    own_bias = lax.dynamic_slice_in_dim(bias_first, me * width, width)
    hidden = causal_conv(edge_mask(act_first), weights_first, own_bias, jnp.bfloat16)

    sums, squares, count = local_stats(hidden.astype(jnp.float32), width // group_size)
    raw_next = chip_gather(with_row_halo(hidden, "hz"), 3)
    sums, squares, count = butterfly_stats(sums, squares, count, ("hz",))
    packed = chip_gather(jnp.stack([sums, squares]), 1)
    mean_chan, scale_chan = group_scale(packed[0], packed[1], count, group_size)
    act_second = activate(raw_next.astype(jnp.float32), mean_chan, scale_chan, gain_second, shift_second)
    own_bias_next = lax.dynamic_slice_in_dim(bias_second, me * width, width)
    branch = causal_conv(edge_mask(act_second), weights_second, own_bias_next, jnp.float32)

    own_latent = lax.dynamic_slice_in_dim(raw_rows[:, 1:-1], me * width, width, axis=3)
    summed = (own_latent.astype(jnp.float32) + branch).astype(jnp.bfloat16)
    summed_rows = scatter_rows(summed, slab_rows, chans)
    return jnp.repeat(jnp.repeat(summed_rows, 2, axis=1), 2, axis=2)


def solution(mesh):
    groups = mesh.shape["groups"]
    height = mesh.shape["height"]
    blocks = CHAN_BLOCKS
    split = Mesh(
        mesh.devices.reshape(groups, height // blocks, 2, blocks // 2),
        ("groups", "hz", "ha", "hb"),
    )
    rows = ("groups", "hz", "ha", "hb")
    slabs = ("hz", "ha", "hb")
    placed = (
        P(None, rows, None, None),
        P(),
        P(),
        P(None, slabs, None),
        P(),
        P(),
        P(),
        P(None, slabs, None),
        P(),
    )
    return jax.shard_map(
        per_device,
        mesh=split,
        in_specs=placed,
        out_specs=P(None, rows, None, None),
        check_vma=False,
    )
```

```python
import jax
import jax.numpy as jnp
from jax import lax
from jax.experimental import pallas as pl
from jax.experimental.pallas import tpu as pltpu
from jax.sharding import Mesh
from jax.sharding import PartitionSpec as P

GROUPS = 32
CHAN_BLOCKS = 4
EPS = 1e-06
HQ = ("ha", "hb")


def shift_pairs(count, step):
    return [(i, (i + step) % count) for i in range(count)]


def butterfly_stats(sums, squares, count, axes):
    for axis in axes:
        size = lax.axis_size(axis)
        bit = 1
        while bit < size:
            pairs = [(i, i ^ bit) for i in range(size)]
            other_sums, other_squares = lax.ppermute((sums, squares), axis, pairs)
            gap = sums - other_sums
            squares = (squares + other_squares) + gap * gap / (2.0 * count)
            sums = sums + other_sums
            count = count * 2
            bit *= 2
    return sums, squares, count


def local_stats(values, groups):
    frames, rows, cols, chans = values.shape
    grouped = values.reshape(frames * rows * cols, groups, chans // groups)
    count = float(frames * rows * cols * (chans // groups))
    sums = jnp.sum(grouped, axis=(0, 2))
    centred = grouped - (sums / count)[None, :, None]
    squares = jnp.sum(centred * centred, axis=(0, 2))
    return sums, squares, count


def group_scale(sums, squares, count, group_size):
    mean = sums / count
    scale = lax.rsqrt(squares / count + EPS)
    return jnp.repeat(mean, group_size), jnp.repeat(scale, group_size)


def activate(values, mean_chan, scale_chan, gain, shift):
    normed = (values - mean_chan) * scale_chan * gain + shift
    return jax.nn.silu(normed).astype(jnp.bfloat16)


def chip_gather(block, dim):
    count_a = lax.axis_size("ha")
    count_b = lax.axis_size("hb")
    me_a = lax.axis_index("ha")
    me_b = lax.axis_index("hb")
    width = block.shape[dim]
    shape = list(block.shape)
    shape[dim] = width * count_a * count_b
    firsts = [block]
    sources = [me_a]
    for step in range(1, count_a):
        firsts.append(lax.ppermute(block, "ha", shift_pairs(count_a, step)))
        sources.append((me_a - step) % count_a)
    firsts = tuple(firsts)
    out = jnp.zeros(shape, block.dtype)
    for step in range(count_b):
        bundle = firsts if step == 0 else lax.ppermute(firsts, "hb", shift_pairs(count_b, step))
        source_b = (me_b - step) % count_b
        for piece, source_a in zip(bundle, sources):
            start = [0] * len(shape)
            start[dim] = (source_a * count_b + source_b) * width
            out = lax.dynamic_update_slice(out, piece, start)
    return out


def edge_mask(cells):
    size = lax.axis_size("hz")
    me = lax.axis_index("hz")
    rows = cells.shape[1]
    row = lax.broadcasted_iota(jnp.int32, (1, rows, 1, 1), 1)
    keep = ((row > 0) | (me > 0)) & ((row < rows - 1) | (me < size - 1))
    return jnp.where(keep, cells, jnp.zeros_like(cells))


def with_row_halo(cells, axis_name):
    size = lax.axis_size(axis_name)
    down = [(i, i + 1) for i in range(size - 1)]
    up = [(i + 1, i) for i in range(size - 1)]
    top = lax.ppermute(cells[:, -1:], axis_name, down)
    bottom = lax.ppermute(cells[:, :1], axis_name, up)
    return jnp.concatenate([top, cells, bottom], axis=1)


def conv_body(x_ref, w_ref, b_ref, o_ref, acc_ref):
    step = pl.program_id(0)
    rows, cols, outs = o_ref.shape[1:]
    chans = x_ref.shape[-1]
    acc_ref[...] = jnp.broadcast_to(b_ref[...], acc_ref.shape)
    for i in range(3):
        for j in range(3):
            for k in range(3):
                patch = x_ref[step + i, pl.ds(j, rows), pl.ds(k, cols), :]
                acc_ref[...] += jnp.dot(
                    patch.reshape(rows * cols, chans),
                    w_ref[9 * i + 3 * j + k],
                    preferred_element_type=jnp.float32,
                )
    o_ref[0] = acc_ref[...].reshape(rows, cols, outs).astype(o_ref.dtype)


def causal_conv(extended, kernel, bias, out_dtype):
    leading = jnp.concatenate([extended[:1], extended[:1], extended], axis=0)
    padded = jnp.pad(leading, ((0, 0), (0, 0), (1, 1), (0, 0)))
    frames = extended.shape[0]
    rows = extended.shape[1] - 2
    cols = extended.shape[2]
    taps, chans, outs = kernel.shape
    flops = 2 * frames * rows * cols * chans * outs * taps
    moved = padded.size * 2 + kernel.size * 2 + frames * rows * cols * outs * 4
    return pl.pallas_call(
        conv_body,
        grid=(frames,),
        in_specs=[
            pl.BlockSpec(padded.shape, lambda t: (0, 0, 0, 0)),
            pl.BlockSpec(kernel.shape, lambda t: (0, 0, 0)),
            pl.BlockSpec((1, outs), lambda t: (0, 0)),
        ],
        out_specs=pl.BlockSpec((1, rows, cols, outs), lambda t: (t, 0, 0, 0)),
        out_shape=jax.ShapeDtypeStruct((frames, rows, cols, outs), out_dtype),
        scratch_shapes=[pltpu.VMEM((rows * cols, outs), jnp.float32)],
        cost_estimate=pl.CostEstimate(flops=flops, bytes_accessed=moved, transcendentals=0),
    )(padded, kernel, bias.reshape(1, outs))


def kernel_block(shard, chans):
    size = lax.axis_size("ha") * lax.axis_size("hb")
    me = lax.axis_index(HQ)
    taps, in_block, outs = shard.shape
    width = outs // size
    out = jnp.zeros((taps, in_block * size, width), shard.dtype)
    for step in range(size):
        target = (me + step) % size
        piece = lax.dynamic_slice_in_dim(shard, target * width, width, axis=2)
        if step:
            piece = lax.ppermute(piece, HQ, shift_pairs(size, step))
        source = (me - step) % size
        out = lax.dynamic_update_slice(out, piece, (0, source * in_block, 0))
    return lax.all_gather(out, "hz", axis=1, tiled=True)


def scatter_rows(branch, slab_rows, chans):
    size = lax.axis_size("ha") * lax.axis_size("hb")
    me = lax.axis_index(HQ)
    frames, rows, cols, width = branch.shape
    out = jnp.zeros((frames, slab_rows, cols, chans), branch.dtype)
    for step in range(size):
        target = (me + step) % size
        piece = lax.dynamic_slice_in_dim(branch, target * slab_rows, slab_rows, axis=1)
        if step:
            piece = lax.ppermute(piece, HQ, shift_pairs(size, step))
        source = (me - step) % size
        out = lax.dynamic_update_slice(out, piece, (0, 0, 0, source * width))
    return out


def per_device(
    latent,
    gain_first,
    shift_first,
    kernel_first,
    bias_first,
    gain_second,
    shift_second,
    kernel_second,
    bias_second,
):
    frames, slab_rows, cols, chans = latent.shape
    blocks = lax.axis_size("ha") * lax.axis_size("hb")
    width = chans // blocks
    me = lax.axis_index(HQ)
    group_size = chans // GROUPS

    weights_first = kernel_block(kernel_first, chans)
    weights_second = kernel_block(kernel_second, chans)

    values = latent.astype(jnp.float32)
    sums, squares, count = local_stats(values, GROUPS)
    raw_rows = with_row_halo(chip_gather(latent, 1), "hz")
    sums, squares, count = butterfly_stats(sums, squares, count, ("ha", "hb", "hz"))
    mean_chan, scale_chan = group_scale(sums, squares, count, group_size)
    act_first = activate(raw_rows.astype(jnp.float32), mean_chan, scale_chan, gain_first, shift_first)
    own_bias = lax.dynamic_slice_in_dim(bias_first, me * width, width)
    hidden = causal_conv(edge_mask(act_first), weights_first, own_bias, jnp.bfloat16)

    sums, squares, count = local_stats(hidden.astype(jnp.float32), width // group_size)
    raw_next = chip_gather(with_row_halo(hidden, "hz"), 3)
    sums, squares, count = butterfly_stats(sums, squares, count, ("hz",))
    packed = chip_gather(jnp.stack([sums, squares]), 1)
    mean_chan, scale_chan = group_scale(packed[0], packed[1], count, group_size)
    act_second = activate(raw_next.astype(jnp.float32), mean_chan, scale_chan, gain_second, shift_second)
    own_bias_next = lax.dynamic_slice_in_dim(bias_second, me * width, width)
    branch = causal_conv(edge_mask(act_second), weights_second, own_bias_next, jnp.float32)

    own_latent = lax.dynamic_slice_in_dim(raw_rows[:, 1:-1], me * width, width, axis=3)
    summed = (own_latent.astype(jnp.float32) + branch).astype(jnp.bfloat16)
    summed_rows = scatter_rows(summed, slab_rows, chans)
    return jnp.repeat(jnp.repeat(summed_rows, 2, axis=1), 2, axis=2)


def solution(mesh):
    groups = mesh.shape["groups"]
    height = mesh.shape["height"]
    blocks = CHAN_BLOCKS
    split = Mesh(
        mesh.devices.reshape(groups, height // blocks, 2, blocks // 2),
        ("groups", "hz", "ha", "hb"),
    )
    rows = ("groups", "hz", "ha", "hb")
    slabs = ("hz", "ha", "hb")
    placed = (
        P(None, rows, None, None),
        P(),
        P(),
        P(None, slabs, None),
        P(),
        P(),
        P(),
        P(None, slabs, None),
        P(),
    )
    return jax.shard_map(
        per_device,
        mesh=split,
        in_specs=placed,
        out_specs=P(None, rows, None, None),
        check_vma=False,
    )
```

```python
import jax
import jax.numpy as jnp
from jax import lax
from jax.experimental import pallas as pl
from jax.experimental.pallas import tpu as pltpu
from jax.sharding import Mesh
from jax.sharding import PartitionSpec as P

GROUPS = 32
CHAN_BLOCKS = 4
EPS = 1e-06
HQ = ("ha", "hb")


def shift_pairs(count, step):
    return [(i, (i + step) % count) for i in range(count)]


def butterfly_stats(sums, squares, count, axes):
    for axis in axes:
        size = lax.axis_size(axis)
        bit = 1
        while bit < size:
            pairs = [(i, i ^ bit) for i in range(size)]
            other_sums, other_squares = lax.ppermute((sums, squares), axis, pairs)
            gap = sums - other_sums
            squares = (squares + other_squares) + gap * gap / (2.0 * count)
            sums = sums + other_sums
            count = count * 2
            bit *= 2
    return sums, squares, count


def local_stats(values, groups):
    frames, rows, cols, chans = values.shape
    grouped = values.reshape(frames * rows * cols, groups, chans // groups)
    count = float(frames * rows * cols * (chans // groups))
    sums = jnp.sum(grouped, axis=(0, 2))
    centred = grouped - (sums / count)[None, :, None]
    squares = jnp.sum(centred * centred, axis=(0, 2))
    return sums, squares, count


def group_scale(sums, squares, count, group_size):
    mean = sums / count
    scale = lax.rsqrt(squares / count + EPS)
    return jnp.repeat(mean, group_size), jnp.repeat(scale, group_size)


def activate(values, mean_chan, scale_chan, gain, shift):
    normed = (values - mean_chan) * scale_chan * gain + shift
    return jax.nn.silu(normed).astype(jnp.bfloat16)


def chip_gather(block, dim):
    count_a = lax.axis_size("ha")
    count_b = lax.axis_size("hb")
    me_a = lax.axis_index("ha")
    me_b = lax.axis_index("hb")
    firsts = [block]
    for step in range(1, count_a):
        firsts.append(lax.ppermute(block, "ha", shift_pairs(count_a, step)))
    firsts = tuple(firsts)
    bundles = [firsts]
    for step in range(1, count_b):
        bundles.append(lax.ppermute(firsts, "hb", shift_pairs(count_b, step)))
    slots = []
    for slot_a in range(count_a):
        for slot_b in range(count_b):
            piece = bundles[0][0]
            for sb in range(count_b):
                for sa in range(count_a):
                    if sa == 0 and sb == 0:
                        continue
                    hit = ((me_a - sa) % count_a == slot_a) & ((me_b - sb) % count_b == slot_b)
                    piece = jnp.where(hit, bundles[sb][sa], piece)
            slots.append(piece)
    return jnp.concatenate(slots, axis=dim)


def edge_mask(cells):
    size = lax.axis_size("hz")
    me = lax.axis_index("hz")
    rows = cells.shape[1]
    row = lax.broadcasted_iota(jnp.int32, (1, rows, 1, 1), 1)
    keep = ((row > 0) | (me > 0)) & ((row < rows - 1) | (me < size - 1))
    return jnp.where(keep, cells, jnp.zeros_like(cells))


def with_row_halo(cells, axis_name):
    size = lax.axis_size(axis_name)
    down = [(i, i + 1) for i in range(size - 1)]
    up = [(i + 1, i) for i in range(size - 1)]
    top = lax.ppermute(cells[:, -1:], axis_name, down)
    bottom = lax.ppermute(cells[:, :1], axis_name, up)
    return jnp.concatenate([top, cells, bottom], axis=1)


def conv_body(x_ref, w_ref, b_ref, o_ref, acc_ref):
    step = pl.program_id(0)
    rows, cols, outs = o_ref.shape[1:]
    chans = x_ref.shape[-1]
    acc_ref[...] = jnp.broadcast_to(b_ref[...], acc_ref.shape)
    for i in range(3):
        for j in range(3):
            for k in range(3):
                patch = x_ref[step + i, pl.ds(j, rows), pl.ds(k, cols), :]
                acc_ref[...] += jnp.dot(
                    patch.reshape(rows * cols, chans),
                    w_ref[9 * i + 3 * j + k],
                    preferred_element_type=jnp.float32,
                )
    o_ref[0] = acc_ref[...].reshape(rows, cols, outs).astype(o_ref.dtype)


def causal_conv(extended, kernel, bias, out_dtype):
    leading = jnp.concatenate([extended[:1], extended[:1], extended], axis=0)
    padded = jnp.pad(leading, ((0, 0), (0, 0), (1, 1), (0, 0)))
    frames = extended.shape[0]
    rows = extended.shape[1] - 2
    cols = extended.shape[2]
    taps, chans, outs = kernel.shape
    flops = 2 * frames * rows * cols * chans * outs * taps
    moved = padded.size * 2 + kernel.size * 2 + frames * rows * cols * outs * 4
    return pl.pallas_call(
        conv_body,
        grid=(frames,),
        in_specs=[
            pl.BlockSpec(padded.shape, lambda t: (0, 0, 0, 0)),
            pl.BlockSpec(kernel.shape, lambda t: (0, 0, 0)),
            pl.BlockSpec((1, outs), lambda t: (0, 0)),
        ],
        out_specs=pl.BlockSpec((1, rows, cols, outs), lambda t: (t, 0, 0, 0)),
        out_shape=jax.ShapeDtypeStruct((frames, rows, cols, outs), out_dtype),
        scratch_shapes=[pltpu.VMEM((rows * cols, outs), jnp.float32)],
        cost_estimate=pl.CostEstimate(flops=flops, bytes_accessed=moved, transcendentals=0),
    )(padded, kernel, bias.reshape(1, outs))


def redistribute(shard):
    size = lax.axis_size("ha") * lax.axis_size("hb")
    me = lax.axis_index(HQ)
    taps, in_block, outs = shard.shape
    width = outs // size
    out = jnp.zeros((taps, in_block * size, width), shard.dtype)
    for step in range(size):
        target = (me + step) % size
        piece = lax.dynamic_slice_in_dim(shard, target * width, width, axis=2)
        if step:
            piece = lax.ppermute(piece, HQ, shift_pairs(size, step))
        source = (me - step) % size
        out = lax.dynamic_update_slice(out, piece, (0, source * in_block, 0))
    return out


def kernel_block(shard, chans):
    return lax.all_gather(redistribute(shard), "hz", axis=1, tiled=True)


def split_block(shard, chans):
    out = redistribute(shard)
    taps, rows_in, width = out.shape
    parts = lax.axis_size("groups")
    part = lax.axis_index("groups")
    rows = lax.axis_size("hz")
    share = rows_in // parts
    mine = lax.dynamic_slice_in_dim(out, part * share, share, axis=1)
    gathered = lax.all_gather(mine, "hz", axis=1)
    received = [gathered]
    for step in range(1, parts):
        received.append(lax.ppermute(gathered, "groups", shift_pairs(parts, step)))
    slots = []
    for slot in range(parts):
        piece = received[0]
        for step in range(1, parts):
            piece = jnp.where((part - step) % parts == slot, received[step], piece)
        slots.append(piece)
    stacked = jnp.stack(slots, axis=2)
    return stacked.reshape(taps, chans, width)


def scatter_rows(branch, slab_rows, chans):
    size = lax.axis_size("ha") * lax.axis_size("hb")
    me = lax.axis_index(HQ)
    frames, rows, cols, width = branch.shape
    out = jnp.zeros((frames, slab_rows, cols, chans), branch.dtype)
    for step in range(size):
        target = (me + step) % size
        piece = lax.dynamic_slice_in_dim(branch, target * slab_rows, slab_rows, axis=1)
        if step:
            piece = lax.ppermute(piece, HQ, shift_pairs(size, step))
        source = (me - step) % size
        out = lax.dynamic_update_slice(out, piece, (0, 0, 0, source * width))
    return out


def per_device(
    latent,
    gain_first,
    shift_first,
    kernel_first,
    bias_first,
    gain_second,
    shift_second,
    kernel_second,
    bias_second,
):
    frames, slab_rows, cols, chans = latent.shape
    blocks = lax.axis_size("ha") * lax.axis_size("hb")
    width = chans // blocks
    me = lax.axis_index(HQ)
    group_size = chans // GROUPS

    weights_first = split_block(kernel_first, chans)
    weights_second = kernel_block(kernel_second, chans)

    values = latent.astype(jnp.float32)
    sums, squares, count = local_stats(values, GROUPS)
    raw_rows = with_row_halo(chip_gather(latent, 1), "hz")
    sums, squares, count = butterfly_stats(sums, squares, count, ("ha", "hb", "hz"))
    mean_chan, scale_chan = group_scale(sums, squares, count, group_size)
    act_first = activate(raw_rows.astype(jnp.float32), mean_chan, scale_chan, gain_first, shift_first)
    own_bias = lax.dynamic_slice_in_dim(bias_first, me * width, width)
    hidden = causal_conv(edge_mask(act_first), weights_first, own_bias, jnp.bfloat16)

    sums, squares, count = local_stats(hidden.astype(jnp.float32), width // group_size)
    raw_next = chip_gather(with_row_halo(hidden, "hz"), 3)
    sums, squares, count = butterfly_stats(sums, squares, count, ("hz",))
    packed = chip_gather(jnp.stack([sums, squares]), 1)
    mean_chan, scale_chan = group_scale(packed[0], packed[1], count, group_size)
    act_second = activate(raw_next.astype(jnp.float32), mean_chan, scale_chan, gain_second, shift_second)
    own_bias_next = lax.dynamic_slice_in_dim(bias_second, me * width, width)
    branch = causal_conv(edge_mask(act_second), weights_second, own_bias_next, jnp.float32)

    own_latent = lax.dynamic_slice_in_dim(raw_rows[:, 1:-1], me * width, width, axis=3)
    summed = (own_latent.astype(jnp.float32) + branch).astype(jnp.bfloat16)
    summed_rows = scatter_rows(summed, slab_rows, chans)
    return jnp.repeat(jnp.repeat(summed_rows, 2, axis=1), 2, axis=2)


def solution(mesh):
    groups = mesh.shape["groups"]
    height = mesh.shape["height"]
    blocks = CHAN_BLOCKS
    split = Mesh(
        mesh.devices.reshape(groups, height // blocks, 2, blocks // 2),
        ("groups", "hz", "ha", "hb"),
    )
    rows = ("groups", "hz", "ha", "hb")
    slabs = ("hz", "ha", "hb")
    placed = (
        P(None, rows, None, None),
        P(),
        P(),
        P(None, slabs, None),
        P(),
        P(),
        P(),
        P(None, slabs, None),
        P(),
    )
    return jax.shard_map(
        per_device,
        mesh=split,
        in_specs=placed,
        out_specs=P(None, rows, None, None),
        check_vma=False,
    )
```

```python
import jax
import jax.numpy as jnp
from jax import lax
from jax.experimental import pallas as pl
from jax.experimental.pallas import tpu as pltpu
from jax.sharding import Mesh
from jax.sharding import PartitionSpec as P

GROUPS = 32
CHAN_BLOCKS = 4
EPS = 1e-06
HQ = ("ha", "hb")


def shift_pairs(count, step):
    return [(i, (i + step) % count) for i in range(count)]


def butterfly_stats(sums, squares, count, axes):
    for axis in axes:
        size = lax.axis_size(axis)
        bit = 1
        while bit < size:
            pairs = [(i, i ^ bit) for i in range(size)]
            other_sums, other_squares = lax.ppermute((sums, squares), axis, pairs)
            gap = sums - other_sums
            squares = (squares + other_squares) + gap * gap / (2.0 * count)
            sums = sums + other_sums
            count = count * 2
            bit *= 2
    return sums, squares, count


def local_stats(values, groups):
    frames, rows, cols, chans = values.shape
    grouped = values.reshape(frames * rows * cols, groups, chans // groups)
    count = float(frames * rows * cols * (chans // groups))
    sums = jnp.sum(grouped, axis=(0, 2))
    centred = grouped - (sums / count)[None, :, None]
    squares = jnp.sum(centred * centred, axis=(0, 2))
    return sums, squares, count


def group_scale(sums, squares, count, group_size):
    mean = sums / count
    scale = lax.rsqrt(squares / count + EPS)
    return jnp.repeat(mean, group_size), jnp.repeat(scale, group_size)


def activate(values, mean_chan, scale_chan, gain, shift):
    normed = (values - mean_chan) * scale_chan * gain + shift
    return jax.nn.silu(normed).astype(jnp.bfloat16)


def chip_gather(block, dim):
    count_a = lax.axis_size("ha")
    count_b = lax.axis_size("hb")
    me_a = lax.axis_index("ha")
    me_b = lax.axis_index("hb")
    width = block.shape[dim]
    shape = list(block.shape)
    shape[dim] = width * count_a * count_b
    firsts = [block]
    sources = [me_a]
    for step in range(1, count_a):
        firsts.append(lax.ppermute(block, "ha", shift_pairs(count_a, step)))
        sources.append((me_a - step) % count_a)
    firsts = tuple(firsts)
    out = jnp.zeros(shape, block.dtype)
    for step in range(count_b):
        bundle = firsts if step == 0 else lax.ppermute(firsts, "hb", shift_pairs(count_b, step))
        source_b = (me_b - step) % count_b
        for piece, source_a in zip(bundle, sources):
            start = [0] * len(shape)
            start[dim] = (source_a * count_b + source_b) * width
            out = lax.dynamic_update_slice(out, piece, start)
    return out


def edge_mask(cells):
    size = lax.axis_size("hz")
    me = lax.axis_index("hz")
    rows = cells.shape[1]
    row = lax.broadcasted_iota(jnp.int32, (1, rows, 1, 1), 1)
    keep = ((row > 0) | (me > 0)) & ((row < rows - 1) | (me < size - 1))
    return jnp.where(keep, cells, jnp.zeros_like(cells))


def with_row_halo(cells, axis_name):
    size = lax.axis_size(axis_name)
    down = [(i, i + 1) for i in range(size - 1)]
    up = [(i + 1, i) for i in range(size - 1)]
    top = lax.ppermute(cells[:, -1:], axis_name, down)
    bottom = lax.ppermute(cells[:, :1], axis_name, up)
    return jnp.concatenate([top, cells, bottom], axis=1)


def conv_body(x_ref, w_ref, b_ref, o_ref, acc_ref):
    frames, rows, cols, outs = o_ref.shape
    chans = x_ref.shape[-1]
    acc_ref[...] = jnp.broadcast_to(b_ref[...], acc_ref.shape)

    def tap_row(index, carry):
        i = index // 3
        j = index % 3
        for k in range(3):
            patch = x_ref[pl.ds(i, frames), pl.ds(j, rows), pl.ds(k, cols), :]
            acc_ref[...] += jnp.dot(
                patch.reshape(frames * rows * cols, chans),
                w_ref[3 * index + k],
                preferred_element_type=jnp.float32,
            )
        return carry

    lax.fori_loop(0, 9, tap_row, 0)
    o_ref[...] = acc_ref[...].reshape(frames, rows, cols, outs).astype(o_ref.dtype)


def causal_conv(extended, kernel, bias, out_dtype):
    leading = jnp.concatenate([extended[:1], extended[:1], extended], axis=0)
    padded = jnp.pad(leading, ((0, 0), (0, 0), (1, 1), (0, 0)))
    frames = extended.shape[0]
    rows = extended.shape[1] - 2
    cols = extended.shape[2]
    taps, chans, outs = kernel.shape
    flops = 2 * frames * rows * cols * chans * outs * taps
    moved = padded.size * 2 + kernel.size * 2 + frames * rows * cols * outs * 4
    return pl.pallas_call(
        conv_body,
        grid=(1,),
        in_specs=[
            pl.BlockSpec(padded.shape, lambda t: (0, 0, 0, 0)),
            pl.BlockSpec(kernel.shape, lambda t: (0, 0, 0)),
            pl.BlockSpec((1, outs), lambda t: (0, 0)),
        ],
        out_specs=pl.BlockSpec((frames, rows, cols, outs), lambda t: (0, 0, 0, 0)),
        out_shape=jax.ShapeDtypeStruct((frames, rows, cols, outs), out_dtype),
        scratch_shapes=[pltpu.VMEM((frames * rows * cols, outs), jnp.float32)],
        cost_estimate=pl.CostEstimate(flops=flops, bytes_accessed=moved, transcendentals=0),
    )(padded, kernel, bias.reshape(1, outs))


def kernel_block(shard, chans):
    size = lax.axis_size("ha") * lax.axis_size("hb")
    me = lax.axis_index(HQ)
    taps, in_block, outs = shard.shape
    width = outs // size
    out = jnp.zeros((taps, in_block * size, width), shard.dtype)
    for step in range(size):
        target = (me + step) % size
        piece = lax.dynamic_slice_in_dim(shard, target * width, width, axis=2)
        if step:
            piece = lax.ppermute(piece, HQ, shift_pairs(size, step))
        source = (me - step) % size
        out = lax.dynamic_update_slice(out, piece, (0, source * in_block, 0))
    return lax.all_gather(out, "hz", axis=1, tiled=True)


def scatter_rows(branch, slab_rows, chans):
    size = lax.axis_size("ha") * lax.axis_size("hb")
    me = lax.axis_index(HQ)
    frames, rows, cols, width = branch.shape
    out = jnp.zeros((frames, slab_rows, cols, chans), branch.dtype)
    for step in range(size):
        target = (me + step) % size
        piece = lax.dynamic_slice_in_dim(branch, target * slab_rows, slab_rows, axis=1)
        if step:
            piece = lax.ppermute(piece, HQ, shift_pairs(size, step))
        source = (me - step) % size
        out = lax.dynamic_update_slice(out, piece, (0, 0, 0, source * width))
    return out


def per_device(
    latent,
    gain_first,
    shift_first,
    kernel_first,
    bias_first,
    gain_second,
    shift_second,
    kernel_second,
    bias_second,
):
    frames, slab_rows, cols, chans = latent.shape
    blocks = lax.axis_size("ha") * lax.axis_size("hb")
    width = chans // blocks
    me = lax.axis_index(HQ)
    group_size = chans // GROUPS

    weights_first = kernel_block(kernel_first, chans)
    weights_second = kernel_block(kernel_second, chans)

    values = latent.astype(jnp.float32)
    sums, squares, count = local_stats(values, GROUPS)
    raw_rows = with_row_halo(chip_gather(latent, 1), "hz")
    sums, squares, count = butterfly_stats(sums, squares, count, ("ha", "hb", "hz"))
    mean_chan, scale_chan = group_scale(sums, squares, count, group_size)
    act_first = activate(raw_rows.astype(jnp.float32), mean_chan, scale_chan, gain_first, shift_first)
    own_bias = lax.dynamic_slice_in_dim(bias_first, me * width, width)
    hidden = causal_conv(edge_mask(act_first), weights_first, own_bias, jnp.bfloat16)

    sums, squares, count = local_stats(hidden.astype(jnp.float32), width // group_size)
    raw_next = chip_gather(with_row_halo(hidden, "hz"), 3)
    sums, squares, count = butterfly_stats(sums, squares, count, ("hz",))
    packed = chip_gather(jnp.stack([sums, squares]), 1)
    mean_chan, scale_chan = group_scale(packed[0], packed[1], count, group_size)
    act_second = activate(raw_next.astype(jnp.float32), mean_chan, scale_chan, gain_second, shift_second)
    own_bias_next = lax.dynamic_slice_in_dim(bias_second, me * width, width)
    branch = causal_conv(edge_mask(act_second), weights_second, own_bias_next, jnp.float32)

    own_latent = lax.dynamic_slice_in_dim(raw_rows[:, 1:-1], me * width, width, axis=3)
    summed = (own_latent.astype(jnp.float32) + branch).astype(jnp.bfloat16)
    summed_rows = scatter_rows(summed, slab_rows, chans)
    return jnp.repeat(jnp.repeat(summed_rows, 2, axis=1), 2, axis=2)


def solution(mesh):
    groups = mesh.shape["groups"]
    height = mesh.shape["height"]
    blocks = CHAN_BLOCKS
    split = Mesh(
        mesh.devices.reshape(groups, height // blocks, 2, blocks // 2),
        ("groups", "hz", "ha", "hb"),
    )
    rows = ("groups", "hz", "ha", "hb")
    slabs = ("hz", "ha", "hb")
    placed = (
        P(None, rows, None, None),
        P(),
        P(),
        P(None, slabs, None),
        P(),
        P(),
        P(),
        P(None, slabs, None),
        P(),
    )
    return jax.shard_map(
        per_device,
        mesh=split,
        in_specs=placed,
        out_specs=P(None, rows, None, None),
        check_vma=False,
    )
```

```python
import jax
import jax.numpy as jnp
from jax import lax
from jax.experimental import pallas as pl
from jax.experimental.pallas import tpu as pltpu
from jax.sharding import Mesh
from jax.sharding import PartitionSpec as P

GROUPS = 32
CHAN_BLOCKS = 4
EPS = 1e-06
HQ = ("ha", "hb")


def shift_pairs(count, step):
    return [(i, (i + step) % count) for i in range(count)]


def butterfly_stats(sums, squares, count, axes):
    for axis in axes:
        size = lax.axis_size(axis)
        bit = 1
        while bit < size:
            pairs = [(i, i ^ bit) for i in range(size)]
            other_sums, other_squares = lax.ppermute((sums, squares), axis, pairs)
            gap = sums - other_sums
            squares = (squares + other_squares) + gap * gap / (2.0 * count)
            sums = sums + other_sums
            count = count * 2
            bit *= 2
    return sums, squares, count


def local_stats(values, groups):
    frames, rows, cols, chans = values.shape
    grouped = values.reshape(frames * rows * cols, groups, chans // groups)
    count = float(frames * rows * cols * (chans // groups))
    sums = jnp.sum(grouped, axis=(0, 2))
    centred = grouped - (sums / count)[None, :, None]
    squares = jnp.sum(centred * centred, axis=(0, 2))
    return sums, squares, count


def group_scale(sums, squares, count, group_size):
    mean = sums / count
    scale = lax.rsqrt(squares / count + EPS)
    return jnp.repeat(mean, group_size), jnp.repeat(scale, group_size)


def activate(values, mean_chan, scale_chan, gain, shift):
    normed = (values - mean_chan) * scale_chan * gain + shift
    return jax.nn.silu(normed).astype(jnp.bfloat16)


def chip_gather(block, dim):
    count_a = lax.axis_size("ha")
    count_b = lax.axis_size("hb")
    me_a = lax.axis_index("ha")
    me_b = lax.axis_index("hb")
    firsts = [block]
    for step in range(1, count_a):
        firsts.append(lax.ppermute(block, "ha", shift_pairs(count_a, step)))
    firsts = tuple(firsts)
    bundles = [firsts]
    for step in range(1, count_b):
        bundles.append(lax.ppermute(firsts, "hb", shift_pairs(count_b, step)))
    slots = []
    for slot_a in range(count_a):
        for slot_b in range(count_b):
            piece = bundles[0][0]
            for sb in range(count_b):
                for sa in range(count_a):
                    if sa == 0 and sb == 0:
                        continue
                    hit = ((me_a - sa) % count_a == slot_a) & ((me_b - sb) % count_b == slot_b)
                    piece = jnp.where(hit, bundles[sb][sa], piece)
            slots.append(piece)
    return jnp.concatenate(slots, axis=dim)


def edge_mask(cells):
    size = lax.axis_size("hz")
    me = lax.axis_index("hz")
    rows = cells.shape[1]
    row = lax.broadcasted_iota(jnp.int32, (1, rows, 1, 1), 1)
    keep = ((row > 0) | (me > 0)) & ((row < rows - 1) | (me < size - 1))
    return jnp.where(keep, cells, jnp.zeros_like(cells))


def with_row_halo(cells, axis_name):
    size = lax.axis_size(axis_name)
    down = [(i, i + 1) for i in range(size - 1)]
    up = [(i + 1, i) for i in range(size - 1)]
    top = lax.ppermute(cells[:, -1:], axis_name, down)
    bottom = lax.ppermute(cells[:, :1], axis_name, up)
    return jnp.concatenate([top, cells, bottom], axis=1)


def conv_body(x_ref, w_ref, b_ref, o_ref, acc_ref):
    step = pl.program_id(0)
    rows, cols, outs = o_ref.shape[1:]
    chans = x_ref.shape[-1]
    acc_ref[...] = jnp.broadcast_to(b_ref[...], acc_ref.shape)
    for i in range(3):
        for j in range(3):
            for k in range(3):
                patch = x_ref[step + i, pl.ds(j, rows), pl.ds(k, cols), :]
                acc_ref[...] += jnp.dot(
                    patch.reshape(rows * cols, chans),
                    w_ref[9 * i + 3 * j + k],
                    preferred_element_type=jnp.float32,
                )
    o_ref[0] = acc_ref[...].reshape(rows, cols, outs).astype(o_ref.dtype)


def causal_conv(extended, kernel, bias, out_dtype):
    leading = jnp.concatenate([extended[:1], extended[:1], extended], axis=0)
    padded = jnp.pad(leading, ((0, 0), (0, 0), (1, 1), (0, 0)))
    frames = extended.shape[0]
    rows = extended.shape[1] - 2
    cols = extended.shape[2]
    taps, chans, outs = kernel.shape
    flops = 2 * frames * rows * cols * chans * outs * taps
    moved = padded.size * 2 + kernel.size * 2 + frames * rows * cols * outs * 4
    return pl.pallas_call(
        conv_body,
        grid=(frames,),
        in_specs=[
            pl.BlockSpec(padded.shape, lambda t: (0, 0, 0, 0)),
            pl.BlockSpec(kernel.shape, lambda t: (0, 0, 0)),
            pl.BlockSpec((1, outs), lambda t: (0, 0)),
        ],
        out_specs=pl.BlockSpec((1, rows, cols, outs), lambda t: (t, 0, 0, 0)),
        out_shape=jax.ShapeDtypeStruct((frames, rows, cols, outs), out_dtype),
        scratch_shapes=[pltpu.VMEM((rows * cols, outs), jnp.float32)],
        cost_estimate=pl.CostEstimate(flops=flops, bytes_accessed=moved, transcendentals=0),
    )(padded, kernel, bias.reshape(1, outs))


def kernel_block(shard, chans):
    count_a = lax.axis_size("ha")
    count_b = lax.axis_size("hb")
    me_a = lax.axis_index("ha")
    me_b = lax.axis_index("hb")
    taps, in_block, outs = shard.shape
    width = outs // (count_a * count_b)
    row_width = width * count_b
    firsts = []
    for step in range(count_a):
        target = (me_a + step) % count_a
        piece = lax.dynamic_slice_in_dim(shard, target * row_width, row_width, axis=2)
        if step:
            piece = lax.ppermute(piece, "ha", shift_pairs(count_a, step))
        firsts.append(piece)
    seconds = []
    for step in range(count_b):
        target = (me_b + step) % count_b
        bundle = tuple(
            lax.dynamic_slice_in_dim(piece, target * width, width, axis=2) for piece in firsts
        )
        if step:
            bundle = lax.ppermute(bundle, "hb", shift_pairs(count_b, step))
        seconds.append(bundle)
    slots = []
    for slot_a in range(count_a):
        for slot_b in range(count_b):
            piece = seconds[0][0]
            for sb in range(count_b):
                for sa in range(count_a):
                    if sa == 0 and sb == 0:
                        continue
                    hit = ((me_a - sa) % count_a == slot_a) & ((me_b - sb) % count_b == slot_b)
                    piece = jnp.where(hit, seconds[sb][sa], piece)
            slots.append(piece)
    out = jnp.concatenate(slots, axis=1)
    return lax.all_gather(out, "hz", axis=1, tiled=True)


def scatter_rows(branch, slab_rows, chans):
    size = lax.axis_size("ha") * lax.axis_size("hb")
    me = lax.axis_index(HQ)
    frames, rows, cols, width = branch.shape
    out = jnp.zeros((frames, slab_rows, cols, chans), branch.dtype)
    for step in range(size):
        target = (me + step) % size
        piece = lax.dynamic_slice_in_dim(branch, target * slab_rows, slab_rows, axis=1)
        if step:
            piece = lax.ppermute(piece, HQ, shift_pairs(size, step))
        source = (me - step) % size
        out = lax.dynamic_update_slice(out, piece, (0, 0, 0, source * width))
    return out


def per_device(
    latent,
    gain_first,
    shift_first,
    kernel_first,
    bias_first,
    gain_second,
    shift_second,
    kernel_second,
    bias_second,
):
    frames, slab_rows, cols, chans = latent.shape
    blocks = lax.axis_size("ha") * lax.axis_size("hb")
    width = chans // blocks
    me = lax.axis_index(HQ)
    group_size = chans // GROUPS

    weights_first = kernel_block(kernel_first, chans)
    weights_second = kernel_block(kernel_second, chans)

    values = latent.astype(jnp.float32)
    sums, squares, count = local_stats(values, GROUPS)
    raw_rows = with_row_halo(chip_gather(latent, 1), "hz")
    sums, squares, count = butterfly_stats(sums, squares, count, ("ha", "hb", "hz"))
    mean_chan, scale_chan = group_scale(sums, squares, count, group_size)
    act_first = activate(raw_rows.astype(jnp.float32), mean_chan, scale_chan, gain_first, shift_first)
    own_bias = lax.dynamic_slice_in_dim(bias_first, me * width, width)
    hidden = causal_conv(edge_mask(act_first), weights_first, own_bias, jnp.bfloat16)

    sums, squares, count = local_stats(hidden.astype(jnp.float32), width // group_size)
    raw_next = chip_gather(with_row_halo(hidden, "hz"), 3)
    sums, squares, count = butterfly_stats(sums, squares, count, ("hz",))
    packed = chip_gather(jnp.stack([sums, squares]), 1)
    mean_chan, scale_chan = group_scale(packed[0], packed[1], count, group_size)
    act_second = activate(raw_next.astype(jnp.float32), mean_chan, scale_chan, gain_second, shift_second)
    own_bias_next = lax.dynamic_slice_in_dim(bias_second, me * width, width)
    branch = causal_conv(edge_mask(act_second), weights_second, own_bias_next, jnp.float32)

    own_latent = lax.dynamic_slice_in_dim(raw_rows[:, 1:-1], me * width, width, axis=3)
    summed = (own_latent.astype(jnp.float32) + branch).astype(jnp.bfloat16)
    summed_rows = scatter_rows(summed, slab_rows, chans)
    return jnp.repeat(jnp.repeat(summed_rows, 2, axis=1), 2, axis=2)


def solution(mesh):
    groups = mesh.shape["groups"]
    height = mesh.shape["height"]
    blocks = CHAN_BLOCKS
    split = Mesh(
        mesh.devices.reshape(groups, height // blocks, 2, blocks // 2),
        ("groups", "hz", "ha", "hb"),
    )
    rows = ("groups", "hz", "ha", "hb")
    slabs = ("hz", "ha", "hb")
    placed = (
        P(None, rows, None, None),
        P(),
        P(),
        P(None, slabs, None),
        P(),
        P(),
        P(),
        P(None, slabs, None),
        P(),
    )
    return jax.shard_map(
        per_device,
        mesh=split,
        in_specs=placed,
        out_specs=P(None, rows, None, None),
        check_vma=False,
    )
```

```python
import jax
import jax.numpy as jnp
from jax import lax
from jax.experimental import pallas as pl
from jax.experimental.pallas import tpu as pltpu
from jax.sharding import Mesh
from jax.sharding import PartitionSpec as P

GROUPS = 32
CHAN_BLOCKS = 4
EPS = 1e-06
HQ = ("ha", "hb")


def shift_pairs(count, step):
    return [(i, (i + step) % count) for i in range(count)]


def butterfly_stats(sums, squares, count, axes):
    for axis in axes:
        size = lax.axis_size(axis)
        bit = 1
        while bit < size:
            pairs = [(i, i ^ bit) for i in range(size)]
            other_sums, other_squares = lax.ppermute((sums, squares), axis, pairs)
            gap = sums - other_sums
            squares = (squares + other_squares) + gap * gap / (2.0 * count)
            sums = sums + other_sums
            count = count * 2
            bit *= 2
    return sums, squares, count


def local_stats(values, groups):
    frames, rows, cols, chans = values.shape
    grouped = values.reshape(frames * rows * cols, groups, chans // groups)
    count = float(frames * rows * cols * (chans // groups))
    sums = jnp.sum(grouped, axis=(0, 2))
    centred = grouped - (sums / count)[None, :, None]
    squares = jnp.sum(centred * centred, axis=(0, 2))
    return sums, squares, count


def group_scale(sums, squares, count, group_size):
    mean = sums / count
    scale = lax.rsqrt(squares / count + EPS)
    return jnp.repeat(mean, group_size), jnp.repeat(scale, group_size)


def activate(values, mean_chan, scale_chan, gain, shift):
    normed = (values - mean_chan) * scale_chan * gain + shift
    return jax.nn.silu(normed).astype(jnp.bfloat16)


def chip_gather(block, dim):
    count_a = lax.axis_size("ha")
    count_b = lax.axis_size("hb")
    me_a = lax.axis_index("ha")
    me_b = lax.axis_index("hb")
    firsts = [block]
    for step in range(1, count_a):
        firsts.append(lax.ppermute(block, "ha", shift_pairs(count_a, step)))
    firsts = tuple(firsts)
    bundles = [firsts]
    for step in range(1, count_b):
        bundles.append(lax.ppermute(firsts, "hb", shift_pairs(count_b, step)))
    slots = []
    for slot_a in range(count_a):
        for slot_b in range(count_b):
            piece = bundles[0][0]
            for sb in range(count_b):
                for sa in range(count_a):
                    if sa == 0 and sb == 0:
                        continue
                    hit = ((me_a - sa) % count_a == slot_a) & ((me_b - sb) % count_b == slot_b)
                    piece = jnp.where(hit, bundles[sb][sa], piece)
            slots.append(piece)
    return jnp.concatenate(slots, axis=dim)


def edge_mask(cells):
    size = lax.axis_size("hz")
    me = lax.axis_index("hz")
    rows = cells.shape[1]
    row = lax.broadcasted_iota(jnp.int32, (1, rows, 1, 1), 1)
    keep = ((row > 0) | (me > 0)) & ((row < rows - 1) | (me < size - 1))
    return jnp.where(keep, cells, jnp.zeros_like(cells))


def with_row_halo(cells, axis_name):
    size = lax.axis_size(axis_name)
    down = [(i, i + 1) for i in range(size - 1)]
    up = [(i + 1, i) for i in range(size - 1)]
    top = lax.ppermute(cells[:, -1:], axis_name, down)
    bottom = lax.ppermute(cells[:, :1], axis_name, up)
    return jnp.concatenate([top, cells, bottom], axis=1)


def conv_body(x_ref, w_ref, b_ref, o_ref, acc_ref):
    step = pl.program_id(0)
    rows, cols, outs = o_ref.shape[1:]
    chans = x_ref.shape[-1]
    acc_ref[...] = jnp.broadcast_to(b_ref[...], acc_ref.shape)
    for i in range(3):
        for j in range(3):
            for k in range(3):
                patch = x_ref[step + i, pl.ds(j, rows), pl.ds(k, cols), :]
                acc_ref[...] += jnp.dot(
                    patch.reshape(rows * cols, chans),
                    w_ref[9 * i + 3 * j + k],
                    preferred_element_type=jnp.float32,
                )
    o_ref[0] = acc_ref[...].reshape(rows, cols, outs).astype(o_ref.dtype)


def causal_conv(extended, kernel, bias, out_dtype):
    leading = jnp.concatenate([extended[:1], extended[:1], extended], axis=0)
    padded = jnp.pad(leading, ((0, 0), (0, 0), (1, 1), (0, 0)))
    frames = extended.shape[0]
    rows = extended.shape[1] - 2
    cols = extended.shape[2]
    taps, chans, outs = kernel.shape
    flops = 2 * frames * rows * cols * chans * outs * taps
    moved = padded.size * 2 + kernel.size * 2 + frames * rows * cols * outs * 4
    return pl.pallas_call(
        conv_body,
        grid=(frames,),
        in_specs=[
            pl.BlockSpec(padded.shape, lambda t: (0, 0, 0, 0)),
            pl.BlockSpec(kernel.shape, lambda t: (0, 0, 0)),
            pl.BlockSpec((1, outs), lambda t: (0, 0)),
        ],
        out_specs=pl.BlockSpec((1, rows, cols, outs), lambda t: (t, 0, 0, 0)),
        out_shape=jax.ShapeDtypeStruct((frames, rows, cols, outs), out_dtype),
        scratch_shapes=[pltpu.VMEM((rows * cols, outs), jnp.float32)],
        cost_estimate=pl.CostEstimate(flops=flops, bytes_accessed=moved, transcendentals=0),
    )(padded, kernel, bias.reshape(1, outs))


def kernel_block(shard, chans, by_permutes=False):
    count_a = lax.axis_size("ha")
    count_b = lax.axis_size("hb")
    me_a = lax.axis_index("ha")
    me_b = lax.axis_index("hb")
    taps, in_block, outs = shard.shape
    width = outs // (count_a * count_b)
    row_width = width * count_b
    firsts = []
    for step in range(count_a):
        target = (me_a + step) % count_a
        piece = lax.dynamic_slice_in_dim(shard, target * row_width, row_width, axis=2)
        if step:
            piece = lax.ppermute(piece, "ha", shift_pairs(count_a, step))
        firsts.append(piece)
    seconds = []
    for step in range(count_b):
        target = (me_b + step) % count_b
        bundle = tuple(
            lax.dynamic_slice_in_dim(piece, target * width, width, axis=2) for piece in firsts
        )
        if step:
            bundle = lax.ppermute(bundle, "hb", shift_pairs(count_b, step))
        seconds.append(bundle)
    slots = []
    for slot_a in range(count_a):
        for slot_b in range(count_b):
            piece = seconds[0][0]
            for sb in range(count_b):
                for sa in range(count_a):
                    if sa == 0 and sb == 0:
                        continue
                    hit = ((me_a - sa) % count_a == slot_a) & ((me_b - sb) % count_b == slot_b)
                    piece = jnp.where(hit, seconds[sb][sa], piece)
            slots.append(piece)
    out = jnp.concatenate(slots, axis=1)
    if not by_permutes:
        return lax.all_gather(out, "hz", axis=1, tiled=True)
    size = lax.axis_size("hz")
    me = lax.axis_index("hz")
    received = [(out, 0)]
    for step in range(1, size):
        down = [(i, i + step) for i in range(size - step)]
        up = [(i + step, i) for i in range(size - step)]
        received.append((lax.ppermute(out, "hz", down), -step))
        received.append((lax.ppermute(out, "hz", up), step))
    slots = []
    for slot in range(size):
        piece = jnp.zeros_like(out)
        for block, offset in received:
            piece = jnp.where(me + offset == slot, block, piece)
        slots.append(piece)
    return jnp.concatenate(slots, axis=1)


def scatter_rows(branch, slab_rows, chans):
    size = lax.axis_size("ha") * lax.axis_size("hb")
    me = lax.axis_index(HQ)
    frames, rows, cols, width = branch.shape
    out = jnp.zeros((frames, slab_rows, cols, chans), branch.dtype)
    for step in range(size):
        target = (me + step) % size
        piece = lax.dynamic_slice_in_dim(branch, target * slab_rows, slab_rows, axis=1)
        if step:
            piece = lax.ppermute(piece, HQ, shift_pairs(size, step))
        source = (me - step) % size
        out = lax.dynamic_update_slice(out, piece, (0, 0, 0, source * width))
    return out


def per_device(
    latent,
    gain_first,
    shift_first,
    kernel_first,
    bias_first,
    gain_second,
    shift_second,
    kernel_second,
    bias_second,
):
    frames, slab_rows, cols, chans = latent.shape
    blocks = lax.axis_size("ha") * lax.axis_size("hb")
    width = chans // blocks
    me = lax.axis_index(HQ)
    group_size = chans // GROUPS

    weights_first = kernel_block(kernel_first, chans)
    weights_second = kernel_block(kernel_second, chans, by_permutes=True)

    values = latent.astype(jnp.float32)
    sums, squares, count = local_stats(values, GROUPS)
    raw_rows = with_row_halo(chip_gather(latent, 1), "hz")
    sums, squares, count = butterfly_stats(sums, squares, count, ("ha", "hb", "hz"))
    mean_chan, scale_chan = group_scale(sums, squares, count, group_size)
    act_first = activate(raw_rows.astype(jnp.float32), mean_chan, scale_chan, gain_first, shift_first)
    own_bias = lax.dynamic_slice_in_dim(bias_first, me * width, width)
    hidden = causal_conv(edge_mask(act_first), weights_first, own_bias, jnp.bfloat16)

    sums, squares, count = local_stats(hidden.astype(jnp.float32), width // group_size)
    raw_next = chip_gather(with_row_halo(hidden, "hz"), 3)
    sums, squares, count = butterfly_stats(sums, squares, count, ("hz",))
    packed = chip_gather(jnp.stack([sums, squares]), 1)
    mean_chan, scale_chan = group_scale(packed[0], packed[1], count, group_size)
    act_second = activate(raw_next.astype(jnp.float32), mean_chan, scale_chan, gain_second, shift_second)
    own_bias_next = lax.dynamic_slice_in_dim(bias_second, me * width, width)
    branch = causal_conv(edge_mask(act_second), weights_second, own_bias_next, jnp.float32)

    own_latent = lax.dynamic_slice_in_dim(raw_rows[:, 1:-1], me * width, width, axis=3)
    summed = (own_latent.astype(jnp.float32) + branch).astype(jnp.bfloat16)
    summed_rows = scatter_rows(summed, slab_rows, chans)
    return jnp.repeat(jnp.repeat(summed_rows, 2, axis=1), 2, axis=2)


def solution(mesh):
    groups = mesh.shape["groups"]
    height = mesh.shape["height"]
    blocks = CHAN_BLOCKS
    split = Mesh(
        mesh.devices.reshape(groups, height // blocks, 2, blocks // 2),
        ("groups", "hz", "ha", "hb"),
    )
    rows = ("groups", "hz", "ha", "hb")
    slabs = ("hz", "ha", "hb")
    placed = (
        P(None, rows, None, None),
        P(),
        P(),
        P(None, slabs, None),
        P(),
        P(),
        P(),
        P(None, slabs, None),
        P(),
    )
    return jax.shard_map(
        per_device,
        mesh=split,
        in_specs=placed,
        out_specs=P(None, rows, None, None),
        check_vma=False,
    )
```

```python
import jax
import jax.numpy as jnp
from jax import lax
from jax.experimental import pallas as pl
from jax.experimental.pallas import tpu as pltpu
from jax.sharding import Mesh
from jax.sharding import PartitionSpec as P

GROUPS = 32
CHAN_BLOCKS = 4
EPS = 1e-06
HQ = ("ha", "hb")


def shift_pairs(count, step):
    return [(i, (i + step) % count) for i in range(count)]


def butterfly_stats(sums, squares, count, axes):
    for axis in axes:
        size = lax.axis_size(axis)
        bit = 1
        while bit < size:
            pairs = [(i, i ^ bit) for i in range(size)]
            other_sums, other_squares = lax.ppermute((sums, squares), axis, pairs)
            gap = sums - other_sums
            squares = (squares + other_squares) + gap * gap / (2.0 * count)
            sums = sums + other_sums
            count = count * 2
            bit *= 2
    return sums, squares, count


def local_stats(values, groups):
    frames, rows, cols, chans = values.shape
    grouped = values.reshape(frames * rows * cols, groups, chans // groups)
    count = float(frames * rows * cols * (chans // groups))
    sums = jnp.sum(grouped, axis=(0, 2))
    centred = grouped - (sums / count)[None, :, None]
    squares = jnp.sum(centred * centred, axis=(0, 2))
    return sums, squares, count


def group_scale(sums, squares, count, group_size):
    mean = sums / count
    scale = lax.rsqrt(squares / count + EPS)
    return jnp.repeat(mean, group_size), jnp.repeat(scale, group_size)


def activate(values, mean_chan, scale_chan, gain, shift):
    normed = (values - mean_chan) * scale_chan * gain + shift
    return jax.nn.silu(normed).astype(jnp.bfloat16)


def chip_gather(block, dim):
    count_a = lax.axis_size("ha")
    count_b = lax.axis_size("hb")
    me_a = lax.axis_index("ha")
    me_b = lax.axis_index("hb")
    firsts = [block]
    for step in range(1, count_a):
        firsts.append(lax.ppermute(block, "ha", shift_pairs(count_a, step)))
    firsts = tuple(firsts)
    bundles = [firsts]
    for step in range(1, count_b):
        bundles.append(lax.ppermute(firsts, "hb", shift_pairs(count_b, step)))
    slots = []
    for slot_a in range(count_a):
        for slot_b in range(count_b):
            piece = bundles[0][0]
            for sb in range(count_b):
                for sa in range(count_a):
                    if sa == 0 and sb == 0:
                        continue
                    hit = ((me_a - sa) % count_a == slot_a) & ((me_b - sb) % count_b == slot_b)
                    piece = jnp.where(hit, bundles[sb][sa], piece)
            slots.append(piece)
    return jnp.concatenate(slots, axis=dim)


def edge_mask(cells):
    size = lax.axis_size("hz")
    me = lax.axis_index("hz")
    rows = cells.shape[1]
    row = lax.broadcasted_iota(jnp.int32, (1, rows, 1, 1), 1)
    keep = ((row > 0) | (me > 0)) & ((row < rows - 1) | (me < size - 1))
    return jnp.where(keep, cells, jnp.zeros_like(cells))


def with_row_halo(cells, axis_name):
    size = lax.axis_size(axis_name)
    down = [(i, i + 1) for i in range(size - 1)]
    up = [(i + 1, i) for i in range(size - 1)]
    top = lax.ppermute(cells[:, -1:], axis_name, down)
    bottom = lax.ppermute(cells[:, :1], axis_name, up)
    return jnp.concatenate([top, cells, bottom], axis=1)


def conv_body(x_ref, w_ref, b_ref, o_ref, acc_ref):
    step = pl.program_id(0)
    rows, cols, outs = o_ref.shape[1:]
    chans = x_ref.shape[-1]
    acc_ref[...] = jnp.broadcast_to(b_ref[...], acc_ref.shape)
    for i in range(3):
        for j in range(3):
            for k in range(3):
                patch = x_ref[step + i, pl.ds(j, rows), pl.ds(k, cols), :]
                acc_ref[...] += jnp.dot(
                    patch.reshape(rows * cols, chans),
                    w_ref[9 * i + 3 * j + k],
                    preferred_element_type=jnp.float32,
                )
    o_ref[0] = acc_ref[...].reshape(rows, cols, outs).astype(o_ref.dtype)


def causal_conv(extended, kernel, bias, out_dtype):
    leading = jnp.concatenate([extended[:1], extended[:1], extended], axis=0)
    padded = jnp.pad(leading, ((0, 0), (0, 0), (1, 1), (0, 0)))
    frames = extended.shape[0]
    rows = extended.shape[1] - 2
    cols = extended.shape[2]
    taps, chans, outs = kernel.shape
    flops = 2 * frames * rows * cols * chans * outs * taps
    moved = padded.size * 2 + kernel.size * 2 + frames * rows * cols * outs * 4
    return pl.pallas_call(
        conv_body,
        grid=(frames,),
        in_specs=[
            pl.BlockSpec(padded.shape, lambda t: (0, 0, 0, 0)),
            pl.BlockSpec(kernel.shape, lambda t: (0, 0, 0)),
            pl.BlockSpec((1, outs), lambda t: (0, 0)),
        ],
        out_specs=pl.BlockSpec((1, rows, cols, outs), lambda t: (t, 0, 0, 0)),
        out_shape=jax.ShapeDtypeStruct((frames, rows, cols, outs), out_dtype),
        scratch_shapes=[pltpu.VMEM((rows * cols, outs), jnp.float32)],
        cost_estimate=pl.CostEstimate(flops=flops, bytes_accessed=moved, transcendentals=0),
    )(padded, kernel, bias.reshape(1, outs))


def kernel_block(shard, chans):
    size = lax.axis_size("ha") * lax.axis_size("hb")
    me = lax.axis_index(HQ)
    taps, in_block, outs = shard.shape
    width = outs // size
    out = jnp.zeros((taps, in_block * size, width), shard.dtype)
    for step in range(size):
        target = (me + step) % size
        piece = lax.dynamic_slice_in_dim(shard, target * width, width, axis=2)
        if step:
            piece = lax.ppermute(piece, HQ, shift_pairs(size, step))
        source = (me - step) % size
        out = lax.dynamic_update_slice(out, piece, (0, source * in_block, 0))
    return lax.all_gather(out, "hz", axis=1, tiled=True)


def scatter_rows(branch, slab_rows, chans):
    size = lax.axis_size("ha") * lax.axis_size("hb")
    me = lax.axis_index(HQ)
    received = []
    for step in range(size):
        target = (me + step) % size
        piece = lax.dynamic_slice_in_dim(branch, target * slab_rows, slab_rows, axis=1)
        if step:
            piece = lax.ppermute(piece, HQ, shift_pairs(size, step))
        received.append(piece)
    slots = []
    for slot in range(size):
        piece = received[0]
        for step in range(1, size):
            piece = jnp.where((me - step) % size == slot, received[step], piece)
        slots.append(piece)
    return jnp.concatenate(slots, axis=3)


def per_device(
    latent,
    gain_first,
    shift_first,
    kernel_first,
    bias_first,
    gain_second,
    shift_second,
    kernel_second,
    bias_second,
):
    frames, slab_rows, cols, chans = latent.shape
    blocks = lax.axis_size("ha") * lax.axis_size("hb")
    width = chans // blocks
    me = lax.axis_index(HQ)
    group_size = chans // GROUPS

    weights_first = kernel_block(kernel_first, chans)
    weights_second = kernel_block(kernel_second, chans)

    values = latent.astype(jnp.float32)
    sums, squares, count = local_stats(values, GROUPS)
    raw_rows = with_row_halo(chip_gather(latent, 1), "hz")
    sums, squares, count = butterfly_stats(sums, squares, count, ("ha", "hb", "hz"))
    mean_chan, scale_chan = group_scale(sums, squares, count, group_size)
    act_first = activate(raw_rows.astype(jnp.float32), mean_chan, scale_chan, gain_first, shift_first)
    own_bias = lax.dynamic_slice_in_dim(bias_first, me * width, width)
    hidden = causal_conv(edge_mask(act_first), weights_first, own_bias, jnp.bfloat16)

    sums, squares, count = local_stats(hidden.astype(jnp.float32), width // group_size)
    raw_next = chip_gather(with_row_halo(hidden, "hz"), 3)
    sums, squares, count = butterfly_stats(sums, squares, count, ("hz",))
    packed = chip_gather(jnp.stack([sums, squares]), 1)
    mean_chan, scale_chan = group_scale(packed[0], packed[1], count, group_size)
    act_second = activate(raw_next.astype(jnp.float32), mean_chan, scale_chan, gain_second, shift_second)
    own_bias_next = lax.dynamic_slice_in_dim(bias_second, me * width, width)
    branch = causal_conv(edge_mask(act_second), weights_second, own_bias_next, jnp.float32)

    own_latent = lax.dynamic_slice_in_dim(raw_rows[:, 1:-1], me * width, width, axis=3)
    summed = (own_latent.astype(jnp.float32) + branch).astype(jnp.bfloat16)
    summed_rows = scatter_rows(summed, slab_rows, chans)
    return jnp.repeat(jnp.repeat(summed_rows, 2, axis=1), 2, axis=2)


def solution(mesh):
    groups = mesh.shape["groups"]
    height = mesh.shape["height"]
    blocks = CHAN_BLOCKS
    split = Mesh(
        mesh.devices.reshape(groups, height // blocks, 2, blocks // 2),
        ("groups", "hz", "ha", "hb"),
    )
    rows = ("groups", "hz", "ha", "hb")
    slabs = ("hz", "ha", "hb")
    placed = (
        P(None, rows, None, None),
        P(),
        P(),
        P(None, slabs, None),
        P(),
        P(),
        P(),
        P(None, slabs, None),
        P(),
    )
    return jax.shard_map(
        per_device,
        mesh=split,
        in_specs=placed,
        out_specs=P(None, rows, None, None),
        check_vma=False,
    )
```

```python
import jax
import jax.numpy as jnp
from jax import lax
from jax.experimental import pallas as pl
from jax.experimental.pallas import tpu as pltpu
from jax.sharding import Mesh
from jax.sharding import PartitionSpec as P

GROUPS = 32
CHAN_BLOCKS = 4
EPS = 1e-06
HQ = ("ha", "hb")


def shift_pairs(count, step):
    return [(i, (i + step) % count) for i in range(count)]


def butterfly_stats(sums, squares, count, axes):
    for axis in axes:
        size = lax.axis_size(axis)
        bit = 1
        while bit < size:
            pairs = [(i, i ^ bit) for i in range(size)]
            other_sums, other_squares = lax.ppermute((sums, squares), axis, pairs)
            gap = sums - other_sums
            squares = (squares + other_squares) + gap * gap / (2.0 * count)
            sums = sums + other_sums
            count = count * 2
            bit *= 2
    return sums, squares, count


def local_stats(values, groups):
    frames, rows, cols, chans = values.shape
    grouped = values.reshape(frames * rows * cols, groups, chans // groups)
    count = float(frames * rows * cols * (chans // groups))
    sums = jnp.sum(grouped, axis=(0, 2))
    centred = grouped - (sums / count)[None, :, None]
    squares = jnp.sum(centred * centred, axis=(0, 2))
    return sums, squares, count


def group_scale(sums, squares, count, group_size):
    mean = sums / count
    scale = lax.rsqrt(squares / count + EPS)
    return jnp.repeat(mean, group_size), jnp.repeat(scale, group_size)


def activate(values, mean_chan, scale_chan, gain, shift):
    normed = (values - mean_chan) * scale_chan * gain + shift
    return jax.nn.silu(normed).astype(jnp.bfloat16)


def chip_gather(block, dim):
    count_a = lax.axis_size("ha")
    count_b = lax.axis_size("hb")
    me_a = lax.axis_index("ha")
    me_b = lax.axis_index("hb")
    firsts = [block]
    for step in range(1, count_a):
        firsts.append(lax.ppermute(block, "ha", shift_pairs(count_a, step)))
    firsts = tuple(firsts)
    bundles = [firsts]
    for step in range(1, count_b):
        bundles.append(lax.ppermute(firsts, "hb", shift_pairs(count_b, step)))
    slots = []
    for slot_a in range(count_a):
        for slot_b in range(count_b):
            piece = bundles[0][0]
            for sb in range(count_b):
                for sa in range(count_a):
                    if sa == 0 and sb == 0:
                        continue
                    hit = ((me_a - sa) % count_a == slot_a) & ((me_b - sb) % count_b == slot_b)
                    piece = jnp.where(hit, bundles[sb][sa], piece)
            slots.append(piece)
    return jnp.concatenate(slots, axis=dim)


def edge_mask(cells):
    size = lax.axis_size("hz")
    me = lax.axis_index("hz")
    rows = cells.shape[1]
    row = lax.broadcasted_iota(jnp.int32, (1, rows, 1, 1), 1)
    keep = ((row > 0) | (me > 0)) & ((row < rows - 1) | (me < size - 1))
    return jnp.where(keep, cells, jnp.zeros_like(cells))


def with_row_halo(cells, axis_name):
    size = lax.axis_size(axis_name)
    down = [(i, i + 1) for i in range(size - 1)]
    up = [(i + 1, i) for i in range(size - 1)]
    top = lax.ppermute(cells[:, -1:], axis_name, down)
    bottom = lax.ppermute(cells[:, :1], axis_name, up)
    return jnp.concatenate([top, cells, bottom], axis=1)


def conv_body(x_ref, w_ref, b_ref, o_ref, acc_ref):
    step = pl.program_id(0)
    rows, cols, outs = o_ref.shape[1:]
    chans = x_ref.shape[-1]
    acc_ref[...] = jnp.broadcast_to(b_ref[...], acc_ref.shape)
    for i in range(3):
        for j in range(3):
            for k in range(3):
                patch = x_ref[k, step + i, pl.ds(j, rows)]
                acc_ref[...] += jnp.dot(
                    patch.reshape(rows * cols, chans),
                    w_ref[9 * i + 3 * j + k],
                    preferred_element_type=jnp.float32,
                )
    o_ref[0] = acc_ref[...].reshape(rows, cols, outs).astype(o_ref.dtype)


def causal_conv(extended, kernel, bias, out_dtype):
    leading = jnp.concatenate([extended[:1], extended[:1], extended], axis=0)
    padded = jnp.pad(leading, ((0, 0), (0, 0), (1, 1), (0, 0)))
    frames = extended.shape[0]
    rows = extended.shape[1] - 2
    cols = extended.shape[2]
    shifted = jnp.stack([padded[:, :, k : k + cols] for k in range(3)])
    taps, chans, outs = kernel.shape
    flops = 2 * frames * rows * cols * chans * outs * taps
    moved = shifted.size * 2 + kernel.size * 2 + frames * rows * cols * outs * 4
    return pl.pallas_call(
        conv_body,
        grid=(frames,),
        in_specs=[
            pl.BlockSpec(shifted.shape, lambda t: (0, 0, 0, 0, 0)),
            pl.BlockSpec(kernel.shape, lambda t: (0, 0, 0)),
            pl.BlockSpec((1, outs), lambda t: (0, 0)),
        ],
        out_specs=pl.BlockSpec((1, rows, cols, outs), lambda t: (t, 0, 0, 0)),
        out_shape=jax.ShapeDtypeStruct((frames, rows, cols, outs), out_dtype),
        scratch_shapes=[pltpu.VMEM((rows * cols, outs), jnp.float32)],
        cost_estimate=pl.CostEstimate(flops=flops, bytes_accessed=moved, transcendentals=0),
    )(shifted, kernel, bias.reshape(1, outs))


def kernel_block(shard, chans):
    size = lax.axis_size("ha") * lax.axis_size("hb")
    me = lax.axis_index(HQ)
    taps, in_block, outs = shard.shape
    width = outs // size
    out = jnp.zeros((taps, in_block * size, width), shard.dtype)
    for step in range(size):
        target = (me + step) % size
        piece = lax.dynamic_slice_in_dim(shard, target * width, width, axis=2)
        if step:
            piece = lax.ppermute(piece, HQ, shift_pairs(size, step))
        source = (me - step) % size
        out = lax.dynamic_update_slice(out, piece, (0, source * in_block, 0))
    return lax.all_gather(out, "hz", axis=1, tiled=True)


def scatter_rows(branch, slab_rows, chans):
    size = lax.axis_size("ha") * lax.axis_size("hb")
    me = lax.axis_index(HQ)
    received = []
    for step in range(size):
        target = (me + step) % size
        piece = lax.dynamic_slice_in_dim(branch, target * slab_rows, slab_rows, axis=1)
        if step:
            piece = lax.ppermute(piece, HQ, shift_pairs(size, step))
        received.append(piece)
    slots = []
    for slot in range(size):
        piece = received[0]
        for step in range(1, size):
            piece = jnp.where((me - step) % size == slot, received[step], piece)
        slots.append(piece)
    return jnp.concatenate(slots, axis=3)


def per_device(
    latent,
    gain_first,
    shift_first,
    kernel_first,
    bias_first,
    gain_second,
    shift_second,
    kernel_second,
    bias_second,
):
    frames, slab_rows, cols, chans = latent.shape
    blocks = lax.axis_size("ha") * lax.axis_size("hb")
    width = chans // blocks
    me = lax.axis_index(HQ)
    group_size = chans // GROUPS

    weights_first = kernel_block(kernel_first, chans)
    weights_second = kernel_block(kernel_second, chans)

    values = latent.astype(jnp.float32)
    sums, squares, count = local_stats(values, GROUPS)
    raw_rows = with_row_halo(chip_gather(latent, 1), "hz")
    sums, squares, count = butterfly_stats(sums, squares, count, ("ha", "hb", "hz"))
    mean_chan, scale_chan = group_scale(sums, squares, count, group_size)
    act_first = activate(raw_rows.astype(jnp.float32), mean_chan, scale_chan, gain_first, shift_first)
    own_bias = lax.dynamic_slice_in_dim(bias_first, me * width, width)
    hidden = causal_conv(edge_mask(act_first), weights_first, own_bias, jnp.bfloat16)

    sums, squares, count = local_stats(hidden.astype(jnp.float32), width // group_size)
    raw_next = chip_gather(with_row_halo(hidden, "hz"), 3)
    sums, squares, count = butterfly_stats(sums, squares, count, ("hz",))
    packed = chip_gather(jnp.stack([sums, squares]), 1)
    mean_chan, scale_chan = group_scale(packed[0], packed[1], count, group_size)
    act_second = activate(raw_next.astype(jnp.float32), mean_chan, scale_chan, gain_second, shift_second)
    own_bias_next = lax.dynamic_slice_in_dim(bias_second, me * width, width)
    branch = causal_conv(edge_mask(act_second), weights_second, own_bias_next, jnp.float32)

    own_latent = lax.dynamic_slice_in_dim(raw_rows[:, 1:-1], me * width, width, axis=3)
    summed = (own_latent.astype(jnp.float32) + branch).astype(jnp.bfloat16)
    summed_rows = scatter_rows(summed, slab_rows, chans)
    return jnp.repeat(jnp.repeat(summed_rows, 2, axis=1), 2, axis=2)


def solution(mesh):
    groups = mesh.shape["groups"]
    height = mesh.shape["height"]
    blocks = CHAN_BLOCKS
    split = Mesh(
        mesh.devices.reshape(groups, height // blocks, 2, blocks // 2),
        ("groups", "hz", "ha", "hb"),
    )
    rows = ("groups", "hz", "ha", "hb")
    slabs = ("hz", "ha", "hb")
    placed = (
        P(None, rows, None, None),
        P(),
        P(),
        P(None, slabs, None),
        P(),
        P(),
        P(),
        P(None, slabs, None),
        P(),
    )
    return jax.shard_map(
        per_device,
        mesh=split,
        in_specs=placed,
        out_specs=P(None, rows, None, None),
        check_vma=False,
    )
```

```python
import jax
import jax.numpy as jnp
from jax import lax
from jax.experimental import pallas as pl
from jax.experimental.pallas import tpu as pltpu
from jax.sharding import Mesh
from jax.sharding import PartitionSpec as P

GROUPS = 32
CHAN_BLOCKS = 4
EPS = 1e-06
HQ = ("ha", "hb")


def shift_pairs(count, step):
    return [(i, (i + step) % count) for i in range(count)]


def butterfly_stats(sums, squares, count, axes):
    for axis in axes:
        size = lax.axis_size(axis)
        bit = 1
        while bit < size:
            pairs = [(i, i ^ bit) for i in range(size)]
            other_sums, other_squares = lax.ppermute((sums, squares), axis, pairs)
            gap = sums - other_sums
            squares = (squares + other_squares) + gap * gap / (2.0 * count)
            sums = sums + other_sums
            count = count * 2
            bit *= 2
    return sums, squares, count


def local_stats(values, groups):
    frames, rows, cols, chans = values.shape
    grouped = values.reshape(frames * rows * cols, groups, chans // groups)
    count = float(frames * rows * cols * (chans // groups))
    sums = jnp.sum(grouped, axis=(0, 2))
    centred = grouped - (sums / count)[None, :, None]
    squares = jnp.sum(centred * centred, axis=(0, 2))
    return sums, squares, count


def group_scale(sums, squares, count, group_size):
    mean = sums / count
    scale = lax.rsqrt(squares / count + EPS)
    return jnp.repeat(mean, group_size), jnp.repeat(scale, group_size)


def activate(values, mean_chan, scale_chan, gain, shift):
    normed = (values - mean_chan) * scale_chan * gain + shift
    return jax.nn.silu(normed).astype(jnp.bfloat16)


def chip_gather(block, dim):
    count_a = lax.axis_size("ha")
    count_b = lax.axis_size("hb")
    me_a = lax.axis_index("ha")
    me_b = lax.axis_index("hb")
    width = block.shape[dim]
    shape = list(block.shape)
    shape[dim] = width * count_a * count_b
    firsts = [block]
    sources = [me_a]
    for step in range(1, count_a):
        firsts.append(lax.ppermute(block, "ha", shift_pairs(count_a, step)))
        sources.append((me_a - step) % count_a)
    firsts = tuple(firsts)
    out = jnp.zeros(shape, block.dtype)
    for step in range(count_b):
        bundle = firsts if step == 0 else lax.ppermute(firsts, "hb", shift_pairs(count_b, step))
        source_b = (me_b - step) % count_b
        for piece, source_a in zip(bundle, sources):
            start = [0] * len(shape)
            start[dim] = (source_a * count_b + source_b) * width
            out = lax.dynamic_update_slice(out, piece, start)
    return out


def edge_mask(cells):
    size = lax.axis_size("hz")
    me = lax.axis_index("hz")
    rows = cells.shape[1]
    row = lax.broadcasted_iota(jnp.int32, (1, rows, 1, 1), 1)
    keep = ((row > 0) | (me > 0)) & ((row < rows - 1) | (me < size - 1))
    return jnp.where(keep, cells, jnp.zeros_like(cells))


def with_row_halo(cells, axis_name):
    size = lax.axis_size(axis_name)
    down = [(i, i + 1) for i in range(size - 1)]
    up = [(i + 1, i) for i in range(size - 1)]
    top = lax.ppermute(cells[:, -1:], axis_name, down)
    bottom = lax.ppermute(cells[:, :1], axis_name, up)
    return jnp.concatenate([top, cells, bottom], axis=1)


def conv_body(x_ref, w_ref, b_ref, o_ref, acc_ref):
    step = pl.program_id(0)
    rows, cols, outs = o_ref.shape[1:]
    chans = x_ref.shape[-1]
    acc_ref[...] = jnp.broadcast_to(b_ref[...], acc_ref.shape)
    for i in range(3):
        for j in range(3):
            for k in range(3):
                patch = x_ref[step + i, pl.ds(j, rows), pl.ds(k, cols), :]
                acc_ref[...] += jnp.dot(
                    patch.reshape(rows * cols, chans),
                    w_ref[9 * i + 3 * j + k],
                    preferred_element_type=jnp.float32,
                )
    o_ref[0] = acc_ref[...].reshape(rows, cols, outs).astype(o_ref.dtype)


def causal_conv(extended, kernel, bias, out_dtype):
    leading = jnp.concatenate([extended[:1], extended[:1], extended], axis=0)
    padded = jnp.pad(leading, ((0, 0), (0, 0), (1, 1), (0, 0)))
    frames = extended.shape[0]
    rows = extended.shape[1] - 2
    cols = extended.shape[2]
    taps, chans, outs = kernel.shape
    flops = 2 * frames * rows * cols * chans * outs * taps
    moved = padded.size * 2 + kernel.size * 2 + frames * rows * cols * outs * 4
    return pl.pallas_call(
        conv_body,
        grid=(frames,),
        in_specs=[
            pl.BlockSpec(padded.shape, lambda t: (0, 0, 0, 0)),
            pl.BlockSpec(kernel.shape, lambda t: (0, 0, 0)),
            pl.BlockSpec((1, outs), lambda t: (0, 0)),
        ],
        out_specs=pl.BlockSpec((1, rows, cols, outs), lambda t: (t, 0, 0, 0)),
        out_shape=jax.ShapeDtypeStruct((frames, rows, cols, outs), out_dtype),
        scratch_shapes=[pltpu.VMEM((rows * cols, outs), jnp.float32)],
        cost_estimate=pl.CostEstimate(flops=flops, bytes_accessed=moved, transcendentals=0),
    )(padded, kernel, bias.reshape(1, outs))


def upsample_body(x_ref, d_ref, o_ref):
    frames, rows = x_ref.shape[:2]
    for t in range(frames):
        for h in range(rows):
            wide = jnp.dot(d_ref[...], x_ref[t, h], preferred_element_type=jnp.float32)
            wide = wide.astype(o_ref.dtype)
            o_ref[t, 2 * h] = wide
            o_ref[t, 2 * h + 1] = wide


def upsample(cells):
    frames, rows, cols, chans = cells.shape
    wide_col = lax.broadcasted_iota(jnp.int32, (2 * cols, cols), 0) // 2
    narrow_col = lax.broadcasted_iota(jnp.int32, (2 * cols, cols), 1)
    dup = (wide_col == narrow_col).astype(cells.dtype)
    return pl.pallas_call(
        upsample_body,
        out_shape=jax.ShapeDtypeStruct((frames, 2 * rows, 2 * cols, chans), cells.dtype),
        in_specs=[
            pl.BlockSpec(memory_space=pltpu.VMEM),
            pl.BlockSpec(memory_space=pltpu.VMEM),
        ],
        out_specs=pl.BlockSpec(memory_space=pltpu.VMEM),
    )(cells, dup)


def kernel_block(shard, chans):
    size = lax.axis_size("ha") * lax.axis_size("hb")
    me = lax.axis_index(HQ)
    taps, in_block, outs = shard.shape
    width = outs // size
    out = jnp.zeros((taps, in_block * size, width), shard.dtype)
    for step in range(size):
        target = (me + step) % size
        piece = lax.dynamic_slice_in_dim(shard, target * width, width, axis=2)
        if step:
            piece = lax.ppermute(piece, HQ, shift_pairs(size, step))
        source = (me - step) % size
        out = lax.dynamic_update_slice(out, piece, (0, source * in_block, 0))
    return lax.all_gather(out, "hz", axis=1, tiled=True)


def scatter_rows(branch, slab_rows, chans):
    size = lax.axis_size("ha") * lax.axis_size("hb")
    me = lax.axis_index(HQ)
    frames, rows, cols, width = branch.shape
    out = jnp.zeros((frames, slab_rows, cols, chans), branch.dtype)
    for step in range(size):
        target = (me + step) % size
        piece = lax.dynamic_slice_in_dim(branch, target * slab_rows, slab_rows, axis=1)
        if step:
            piece = lax.ppermute(piece, HQ, shift_pairs(size, step))
        source = (me - step) % size
        out = lax.dynamic_update_slice(out, piece, (0, 0, 0, source * width))
    return out


def per_device(
    latent,
    gain_first,
    shift_first,
    kernel_first,
    bias_first,
    gain_second,
    shift_second,
    kernel_second,
    bias_second,
):
    frames, slab_rows, cols, chans = latent.shape
    blocks = lax.axis_size("ha") * lax.axis_size("hb")
    width = chans // blocks
    me = lax.axis_index(HQ)
    group_size = chans // GROUPS

    weights_first = kernel_block(kernel_first, chans)
    weights_second = kernel_block(kernel_second, chans)

    values = latent.astype(jnp.float32)
    sums, squares, count = local_stats(values, GROUPS)
    raw_rows = with_row_halo(chip_gather(latent, 1), "hz")
    sums, squares, count = butterfly_stats(sums, squares, count, ("ha", "hb", "hz"))
    mean_chan, scale_chan = group_scale(sums, squares, count, group_size)
    act_first = activate(raw_rows.astype(jnp.float32), mean_chan, scale_chan, gain_first, shift_first)
    own_bias = lax.dynamic_slice_in_dim(bias_first, me * width, width)
    hidden = causal_conv(edge_mask(act_first), weights_first, own_bias, jnp.bfloat16)

    sums, squares, count = local_stats(hidden.astype(jnp.float32), width // group_size)
    raw_next = chip_gather(with_row_halo(hidden, "hz"), 3)
    sums, squares, count = butterfly_stats(sums, squares, count, ("hz",))
    packed = chip_gather(jnp.stack([sums, squares]), 1)
    mean_chan, scale_chan = group_scale(packed[0], packed[1], count, group_size)
    act_second = activate(raw_next.astype(jnp.float32), mean_chan, scale_chan, gain_second, shift_second)
    own_bias_next = lax.dynamic_slice_in_dim(bias_second, me * width, width)
    branch = causal_conv(edge_mask(act_second), weights_second, own_bias_next, jnp.float32)

    own_latent = lax.dynamic_slice_in_dim(raw_rows[:, 1:-1], me * width, width, axis=3)
    summed = (own_latent.astype(jnp.float32) + branch).astype(jnp.bfloat16)
    summed_rows = scatter_rows(summed, slab_rows, chans)
    return upsample(summed_rows)


def solution(mesh):
    groups = mesh.shape["groups"]
    height = mesh.shape["height"]
    blocks = CHAN_BLOCKS
    split = Mesh(
        mesh.devices.reshape(groups, height // blocks, 2, blocks // 2),
        ("groups", "hz", "ha", "hb"),
    )
    rows = ("groups", "hz", "ha", "hb")
    slabs = ("hz", "ha", "hb")
    placed = (
        P(None, rows, None, None),
        P(),
        P(),
        P(None, slabs, None),
        P(),
        P(),
        P(),
        P(None, slabs, None),
        P(),
    )
    return jax.shard_map(
        per_device,
        mesh=split,
        in_specs=placed,
        out_specs=P(None, rows, None, None),
        check_vma=False,
    )
```

```python
import jax
import jax.numpy as jnp
from jax import lax
from jax.experimental import pallas as pl
from jax.experimental.pallas import tpu as pltpu
from jax.sharding import Mesh
from jax.sharding import PartitionSpec as P

GROUPS = 32
CHAN_BLOCKS = 4
EPS = 1e-06
HQ = ("ha", "hb")


def shift_pairs(count, step):
    return [(i, (i + step) % count) for i in range(count)]


def butterfly_stats(sums, squares, count, axes):
    for axis in axes:
        size = lax.axis_size(axis)
        bit = 1
        while bit < size:
            pairs = [(i, i ^ bit) for i in range(size)]
            other_sums, other_squares = lax.ppermute((sums, squares), axis, pairs)
            gap = sums - other_sums
            squares = (squares + other_squares) + gap * gap / (2.0 * count)
            sums = sums + other_sums
            count = count * 2
            bit *= 2
    return sums, squares, count


def local_stats(values, groups):
    frames, rows, cols, chans = values.shape
    grouped = values.reshape(frames * rows * cols, groups, chans // groups)
    count = float(frames * rows * cols * (chans // groups))
    sums = jnp.sum(grouped, axis=(0, 2))
    centred = grouped - (sums / count)[None, :, None]
    squares = jnp.sum(centred * centred, axis=(0, 2))
    return sums, squares, count


def group_scale(sums, squares, count, group_size):
    mean = sums / count
    scale = lax.rsqrt(squares / count + EPS)
    return jnp.repeat(mean, group_size), jnp.repeat(scale, group_size)


def activate(values, mean_chan, scale_chan, gain, shift):
    normed = (values - mean_chan) * scale_chan * gain + shift
    return jax.nn.silu(normed).astype(jnp.bfloat16)


def chip_gather(block, dim):
    count_a = lax.axis_size("ha")
    count_b = lax.axis_size("hb")
    me_a = lax.axis_index("ha")
    me_b = lax.axis_index("hb")
    width = block.shape[dim]
    shape = list(block.shape)
    shape[dim] = width * count_a * count_b
    firsts = [block]
    sources = [me_a]
    for step in range(1, count_a):
        firsts.append(lax.ppermute(block, "ha", shift_pairs(count_a, step)))
        sources.append((me_a - step) % count_a)
    firsts = tuple(firsts)
    out = jnp.zeros(shape, block.dtype)
    for step in range(count_b):
        bundle = firsts if step == 0 else lax.ppermute(firsts, "hb", shift_pairs(count_b, step))
        source_b = (me_b - step) % count_b
        for piece, source_a in zip(bundle, sources):
            start = [0] * len(shape)
            start[dim] = (source_a * count_b + source_b) * width
            out = lax.dynamic_update_slice(out, piece, start)
    return out


def edge_mask(cells):
    size = lax.axis_size("hz")
    me = lax.axis_index("hz")
    rows = cells.shape[1]
    row = lax.broadcasted_iota(jnp.int32, (1, rows, 1, 1), 1)
    keep = ((row > 0) | (me > 0)) & ((row < rows - 1) | (me < size - 1))
    return jnp.where(keep, cells, jnp.zeros_like(cells))


def with_row_halo(cells, axis_name):
    size = lax.axis_size(axis_name)
    down = [(i, i + 1) for i in range(size - 1)]
    up = [(i + 1, i) for i in range(size - 1)]
    top = lax.ppermute(cells[:, -1:], axis_name, down)
    bottom = lax.ppermute(cells[:, :1], axis_name, up)
    return jnp.concatenate([top, cells, bottom], axis=1)


def conv_body(x_ref, w_ref, b_ref, o_ref, acc_ref):
    tap_row = pl.program_id(0)
    frame = pl.program_id(1)
    frames, rows, cols, outs = o_ref.shape
    chans = x_ref.shape[-1]

    @pl.when(tap_row == 0)
    def _():
        acc_ref[frame] = jnp.broadcast_to(b_ref[...], acc_ref.shape[1:])

    for j in range(3):
        for k in range(3):
            patch = x_ref[0, pl.ds(j, rows), pl.ds(k, cols), :]
            acc_ref[frame] += jnp.dot(
                patch.reshape(rows * cols, chans),
                w_ref[3 * j + k],
                preferred_element_type=jnp.float32,
            )

    @pl.when(tap_row == 2)
    def _():
        o_ref[frame] = acc_ref[frame].reshape(rows, cols, outs).astype(o_ref.dtype)


def causal_conv(extended, kernel, bias, out_dtype):
    leading = jnp.concatenate([extended[:1], extended[:1], extended], axis=0)
    padded = jnp.pad(leading, ((0, 0), (0, 0), (1, 1), (0, 0)))
    frames = extended.shape[0]
    rows = extended.shape[1] - 2
    cols = extended.shape[2]
    taps, chans, outs = kernel.shape
    flops = 2 * frames * rows * cols * chans * outs * taps
    moved = padded.size * 2 * 3 // 5 * 3 + kernel.size * 2 + frames * rows * cols * outs * 4
    return pl.pallas_call(
        conv_body,
        grid=(3, frames),
        in_specs=[
            pl.BlockSpec((1,) + padded.shape[1:], lambda i, t: (t + i, 0, 0, 0)),
            pl.BlockSpec((9, chans, outs), lambda i, t: (i, 0, 0)),
            pl.BlockSpec((1, outs), lambda i, t: (0, 0)),
        ],
        out_specs=pl.BlockSpec((frames, rows, cols, outs), lambda i, t: (0, 0, 0, 0)),
        out_shape=jax.ShapeDtypeStruct((frames, rows, cols, outs), out_dtype),
        scratch_shapes=[pltpu.VMEM((frames, rows * cols, outs), jnp.float32)],
        cost_estimate=pl.CostEstimate(flops=flops, bytes_accessed=moved, transcendentals=0),
    )(padded, kernel, bias.reshape(1, outs))


def kernel_block(shard, chans):
    size = lax.axis_size("ha") * lax.axis_size("hb")
    me = lax.axis_index(HQ)
    taps, in_block, outs = shard.shape
    width = outs // size
    out = jnp.zeros((taps, in_block * size, width), shard.dtype)
    for step in range(size):
        target = (me + step) % size
        piece = lax.dynamic_slice_in_dim(shard, target * width, width, axis=2)
        if step:
            piece = lax.ppermute(piece, HQ, shift_pairs(size, step))
        source = (me - step) % size
        out = lax.dynamic_update_slice(out, piece, (0, source * in_block, 0))
    return lax.all_gather(out, "hz", axis=1, tiled=True)


def scatter_rows(branch, slab_rows, chans):
    size = lax.axis_size("ha") * lax.axis_size("hb")
    me = lax.axis_index(HQ)
    frames, rows, cols, width = branch.shape
    out = jnp.zeros((frames, slab_rows, cols, chans), branch.dtype)
    for step in range(size):
        target = (me + step) % size
        piece = lax.dynamic_slice_in_dim(branch, target * slab_rows, slab_rows, axis=1)
        if step:
            piece = lax.ppermute(piece, HQ, shift_pairs(size, step))
        source = (me - step) % size
        out = lax.dynamic_update_slice(out, piece, (0, 0, 0, source * width))
    return out


def per_device(
    latent,
    gain_first,
    shift_first,
    kernel_first,
    bias_first,
    gain_second,
    shift_second,
    kernel_second,
    bias_second,
):
    frames, slab_rows, cols, chans = latent.shape
    blocks = lax.axis_size("ha") * lax.axis_size("hb")
    width = chans // blocks
    me = lax.axis_index(HQ)
    group_size = chans // GROUPS

    weights_first = kernel_block(kernel_first, chans)
    weights_second = kernel_block(kernel_second, chans)

    values = latent.astype(jnp.float32)
    sums, squares, count = local_stats(values, GROUPS)
    raw_rows = with_row_halo(chip_gather(latent, 1), "hz")
    sums, squares, count = butterfly_stats(sums, squares, count, ("ha", "hb", "hz"))
    mean_chan, scale_chan = group_scale(sums, squares, count, group_size)
    act_first = activate(raw_rows.astype(jnp.float32), mean_chan, scale_chan, gain_first, shift_first)
    own_bias = lax.dynamic_slice_in_dim(bias_first, me * width, width)
    hidden = causal_conv(edge_mask(act_first), weights_first, own_bias, jnp.bfloat16)

    sums, squares, count = local_stats(hidden.astype(jnp.float32), width // group_size)
    raw_next = chip_gather(with_row_halo(hidden, "hz"), 3)
    sums, squares, count = butterfly_stats(sums, squares, count, ("hz",))
    packed = chip_gather(jnp.stack([sums, squares]), 1)
    mean_chan, scale_chan = group_scale(packed[0], packed[1], count, group_size)
    act_second = activate(raw_next.astype(jnp.float32), mean_chan, scale_chan, gain_second, shift_second)
    own_bias_next = lax.dynamic_slice_in_dim(bias_second, me * width, width)
    branch = causal_conv(edge_mask(act_second), weights_second, own_bias_next, jnp.float32)

    own_latent = lax.dynamic_slice_in_dim(raw_rows[:, 1:-1], me * width, width, axis=3)
    summed = (own_latent.astype(jnp.float32) + branch).astype(jnp.bfloat16)
    summed_rows = scatter_rows(summed, slab_rows, chans)
    return jnp.repeat(jnp.repeat(summed_rows, 2, axis=1), 2, axis=2)


def solution(mesh):
    groups = mesh.shape["groups"]
    height = mesh.shape["height"]
    blocks = CHAN_BLOCKS
    split = Mesh(
        mesh.devices.reshape(groups, height // blocks, 2, blocks // 2),
        ("groups", "hz", "ha", "hb"),
    )
    rows = ("groups", "hz", "ha", "hb")
    slabs = ("hz", "ha", "hb")
    placed = (
        P(None, rows, None, None),
        P(),
        P(),
        P(None, slabs, None),
        P(),
        P(),
        P(),
        P(None, slabs, None),
        P(),
    )
    return jax.shard_map(
        per_device,
        mesh=split,
        in_specs=placed,
        out_specs=P(None, rows, None, None),
        check_vma=False,
    )
```

```python
import jax
import jax.numpy as jnp
from jax import lax
from jax.experimental import pallas as pl
from jax.experimental.pallas import tpu as pltpu
from jax.sharding import Mesh
from jax.sharding import PartitionSpec as P

GROUPS = 32
CHAN_BLOCKS = 4
EPS = 1e-06
HQ = ("ha", "hb")


def shift_pairs(count, step):
    return [(i, (i + step) % count) for i in range(count)]


def butterfly_stats(sums, squares, count, axes):
    for axis in axes:
        size = lax.axis_size(axis)
        bit = 1
        while bit < size:
            pairs = [(i, i ^ bit) for i in range(size)]
            other_sums, other_squares = lax.ppermute((sums, squares), axis, pairs)
            gap = sums - other_sums
            squares = (squares + other_squares) + gap * gap / (2.0 * count)
            sums = sums + other_sums
            count = count * 2
            bit *= 2
    return sums, squares, count


def local_stats(values, groups):
    frames, rows, cols, chans = values.shape
    grouped = values.reshape(frames * rows * cols, groups, chans // groups)
    count = float(frames * rows * cols * (chans // groups))
    sums = jnp.sum(grouped, axis=(0, 2))
    centred = grouped - (sums / count)[None, :, None]
    squares = jnp.sum(centred * centred, axis=(0, 2))
    return sums, squares, count


def group_scale(sums, squares, count, group_size):
    mean = sums / count
    scale = lax.rsqrt(squares / count + EPS)
    return jnp.repeat(mean, group_size), jnp.repeat(scale, group_size)


def activate(values, mean_chan, scale_chan, gain, shift):
    normed = (values - mean_chan) * scale_chan * gain + shift
    return jax.nn.silu(normed).astype(jnp.bfloat16)


def chip_gather(block, dim):
    count_a = lax.axis_size("ha")
    count_b = lax.axis_size("hb")
    me_a = lax.axis_index("ha")
    me_b = lax.axis_index("hb")
    width = block.shape[dim]
    shape = list(block.shape)
    shape[dim] = width * count_a * count_b
    firsts = [block]
    sources = [me_a]
    for step in range(1, count_a):
        firsts.append(lax.ppermute(block, "ha", shift_pairs(count_a, step)))
        sources.append((me_a - step) % count_a)
    firsts = tuple(firsts)
    out = jnp.zeros(shape, block.dtype)
    for step in range(count_b):
        bundle = firsts if step == 0 else lax.ppermute(firsts, "hb", shift_pairs(count_b, step))
        source_b = (me_b - step) % count_b
        for piece, source_a in zip(bundle, sources):
            start = [0] * len(shape)
            start[dim] = (source_a * count_b + source_b) * width
            out = lax.dynamic_update_slice(out, piece, start)
    return out


def edge_mask(cells):
    size = lax.axis_size("hz")
    me = lax.axis_index("hz")
    rows = cells.shape[1]
    row = lax.broadcasted_iota(jnp.int32, (1, rows, 1, 1), 1)
    keep = ((row > 0) | (me > 0)) & ((row < rows - 1) | (me < size - 1))
    return jnp.where(keep, cells, jnp.zeros_like(cells))


def with_row_halo(cells, axis_name):
    size = lax.axis_size(axis_name)
    down = [(i, i + 1) for i in range(size - 1)]
    up = [(i + 1, i) for i in range(size - 1)]
    top = lax.ppermute(cells[:, -1:], axis_name, down)
    bottom = lax.ppermute(cells[:, :1], axis_name, up)
    return jnp.concatenate([top, cells, bottom], axis=1)


def conv_body(x_ref, w_ref, b_ref, o_ref, acc_ref):
    step = pl.program_id(0)
    rows, cols, outs = o_ref.shape[1:]
    chans = x_ref.shape[-1]
    part = rows // 2
    for half in range(2):
        first = half * part
        total = jnp.broadcast_to(b_ref[...], (part * cols, outs))
        for i in range(3):
            for j in range(3):
                for k in range(3):
                    patch = x_ref[step + i, pl.ds(first + j, part), pl.ds(k, cols), :]
                    total = total + jnp.dot(
                        patch.reshape(part * cols, chans),
                        w_ref[9 * i + 3 * j + k],
                        preferred_element_type=jnp.float32,
                    )
        o_ref[0, pl.ds(first, part)] = total.reshape(part, cols, outs).astype(o_ref.dtype)


def causal_conv(extended, kernel, bias, out_dtype):
    leading = jnp.concatenate([extended[:1], extended[:1], extended], axis=0)
    padded = jnp.pad(leading, ((0, 0), (0, 0), (1, 1), (0, 0)))
    frames = extended.shape[0]
    rows = extended.shape[1] - 2
    cols = extended.shape[2]
    taps, chans, outs = kernel.shape
    flops = 2 * frames * rows * cols * chans * outs * taps
    moved = padded.size * 2 + kernel.size * 2 + frames * rows * cols * outs * 4
    return pl.pallas_call(
        conv_body,
        grid=(frames,),
        in_specs=[
            pl.BlockSpec(padded.shape, lambda t: (0, 0, 0, 0)),
            pl.BlockSpec(kernel.shape, lambda t: (0, 0, 0)),
            pl.BlockSpec((1, outs), lambda t: (0, 0)),
        ],
        out_specs=pl.BlockSpec((1, rows, cols, outs), lambda t: (t, 0, 0, 0)),
        out_shape=jax.ShapeDtypeStruct((frames, rows, cols, outs), out_dtype),
        scratch_shapes=[pltpu.VMEM((rows * cols, outs), jnp.float32)],
        cost_estimate=pl.CostEstimate(flops=flops, bytes_accessed=moved, transcendentals=0),
    )(padded, kernel, bias.reshape(1, outs))


def kernel_block(shard, chans):
    size = lax.axis_size("ha") * lax.axis_size("hb")
    me = lax.axis_index(HQ)
    taps, in_block, outs = shard.shape
    width = outs // size
    out = jnp.zeros((taps, in_block * size, width), shard.dtype)
    for step in range(size):
        target = (me + step) % size
        piece = lax.dynamic_slice_in_dim(shard, target * width, width, axis=2)
        if step:
            piece = lax.ppermute(piece, HQ, shift_pairs(size, step))
        source = (me - step) % size
        out = lax.dynamic_update_slice(out, piece, (0, source * in_block, 0))
    return lax.all_gather(out, "hz", axis=1, tiled=True)


def scatter_rows(branch, slab_rows, chans):
    size = lax.axis_size("ha") * lax.axis_size("hb")
    me = lax.axis_index(HQ)
    frames, rows, cols, width = branch.shape
    out = jnp.zeros((frames, slab_rows, cols, chans), branch.dtype)
    for step in range(size):
        target = (me + step) % size
        piece = lax.dynamic_slice_in_dim(branch, target * slab_rows, slab_rows, axis=1)
        if step:
            piece = lax.ppermute(piece, HQ, shift_pairs(size, step))
        source = (me - step) % size
        out = lax.dynamic_update_slice(out, piece, (0, 0, 0, source * width))
    return out


def per_device(
    latent,
    gain_first,
    shift_first,
    kernel_first,
    bias_first,
    gain_second,
    shift_second,
    kernel_second,
    bias_second,
):
    frames, slab_rows, cols, chans = latent.shape
    blocks = lax.axis_size("ha") * lax.axis_size("hb")
    width = chans // blocks
    me = lax.axis_index(HQ)
    group_size = chans // GROUPS

    weights_first = kernel_block(kernel_first, chans)
    weights_second = kernel_block(kernel_second, chans)

    values = latent.astype(jnp.float32)
    sums, squares, count = local_stats(values, GROUPS)
    raw_rows = with_row_halo(chip_gather(latent, 1), "hz")
    sums, squares, count = butterfly_stats(sums, squares, count, ("ha", "hb", "hz"))
    mean_chan, scale_chan = group_scale(sums, squares, count, group_size)
    act_first = activate(raw_rows.astype(jnp.float32), mean_chan, scale_chan, gain_first, shift_first)
    own_bias = lax.dynamic_slice_in_dim(bias_first, me * width, width)
    hidden = causal_conv(edge_mask(act_first), weights_first, own_bias, jnp.bfloat16)

    sums, squares, count = local_stats(hidden.astype(jnp.float32), width // group_size)
    raw_next = chip_gather(with_row_halo(hidden, "hz"), 3)
    sums, squares, count = butterfly_stats(sums, squares, count, ("hz",))
    packed = chip_gather(jnp.stack([sums, squares]), 1)
    mean_chan, scale_chan = group_scale(packed[0], packed[1], count, group_size)
    act_second = activate(raw_next.astype(jnp.float32), mean_chan, scale_chan, gain_second, shift_second)
    own_bias_next = lax.dynamic_slice_in_dim(bias_second, me * width, width)
    branch = causal_conv(edge_mask(act_second), weights_second, own_bias_next, jnp.float32)

    own_latent = lax.dynamic_slice_in_dim(raw_rows[:, 1:-1], me * width, width, axis=3)
    summed = (own_latent.astype(jnp.float32) + branch).astype(jnp.bfloat16)
    summed_rows = scatter_rows(summed, slab_rows, chans)
    return jnp.repeat(jnp.repeat(summed_rows, 2, axis=1), 2, axis=2)


def solution(mesh):
    groups = mesh.shape["groups"]
    height = mesh.shape["height"]
    blocks = CHAN_BLOCKS
    split = Mesh(
        mesh.devices.reshape(groups, height // blocks, 2, blocks // 2),
        ("groups", "hz", "ha", "hb"),
    )
    rows = ("groups", "hz", "ha", "hb")
    slabs = ("hz", "ha", "hb")
    placed = (
        P(None, rows, None, None),
        P(),
        P(),
        P(None, slabs, None),
        P(),
        P(),
        P(),
        P(None, slabs, None),
        P(),
    )
    return jax.shard_map(
        per_device,
        mesh=split,
        in_specs=placed,
        out_specs=P(None, rows, None, None),
        check_vma=False,
    )
```

```python
import jax
import jax.numpy as jnp
from jax import lax
from jax.experimental import pallas as pl
from jax.experimental.pallas import tpu as pltpu
from jax.sharding import Mesh
from jax.sharding import PartitionSpec as P

GROUPS = 32
CHAN_BLOCKS = 4
EPS = 1e-06
HQ = ("ha", "hb")


def shift_pairs(count, step):
    return [(i, (i + step) % count) for i in range(count)]


def butterfly_stats(sums, squares, count, axes):
    for axis in axes:
        size = lax.axis_size(axis)
        bit = 1
        while bit < size:
            pairs = [(i, i ^ bit) for i in range(size)]
            other_sums, other_squares = lax.ppermute((sums, squares), axis, pairs)
            gap = sums - other_sums
            squares = (squares + other_squares) + gap * gap / (2.0 * count)
            sums = sums + other_sums
            count = count * 2
            bit *= 2
    return sums, squares, count


def local_stats(values, groups):
    frames, rows, cols, chans = values.shape
    grouped = values.reshape(frames * rows * cols, groups, chans // groups)
    count = float(frames * rows * cols * (chans // groups))
    sums = jnp.sum(grouped, axis=(0, 2))
    centred = grouped - (sums / count)[None, :, None]
    squares = jnp.sum(centred * centred, axis=(0, 2))
    return sums, squares, count


def group_scale(sums, squares, count, group_size):
    mean = sums / count
    scale = lax.rsqrt(squares / count + EPS)
    return jnp.repeat(mean, group_size), jnp.repeat(scale, group_size)


def activate(values, mean_chan, scale_chan, gain, shift):
    normed = (values - mean_chan) * scale_chan * gain + shift
    return jax.nn.silu(normed).astype(jnp.bfloat16)


def chip_gather(block, dim):
    count_a = lax.axis_size("ha")
    count_b = lax.axis_size("hb")
    me_a = lax.axis_index("ha")
    me_b = lax.axis_index("hb")
    width = block.shape[dim]
    shape = list(block.shape)
    shape[dim] = width * count_a * count_b
    firsts = [block]
    sources = [me_a]
    for step in range(1, count_a):
        firsts.append(lax.ppermute(block, "ha", shift_pairs(count_a, step)))
        sources.append((me_a - step) % count_a)
    firsts = tuple(firsts)
    out = jnp.zeros(shape, block.dtype)
    for step in range(count_b):
        bundle = firsts if step == 0 else lax.ppermute(firsts, "hb", shift_pairs(count_b, step))
        source_b = (me_b - step) % count_b
        for piece, source_a in zip(bundle, sources):
            start = [0] * len(shape)
            start[dim] = (source_a * count_b + source_b) * width
            out = lax.dynamic_update_slice(out, piece, start)
    return out


def edge_mask(cells):
    size = lax.axis_size("hz")
    me = lax.axis_index("hz")
    rows = cells.shape[1]
    row = lax.broadcasted_iota(jnp.int32, (1, rows, 1, 1), 1)
    keep = ((row > 0) | (me > 0)) & ((row < rows - 1) | (me < size - 1))
    return jnp.where(keep, cells, jnp.zeros_like(cells))


def with_row_halo(cells, axis_name):
    size = lax.axis_size(axis_name)
    down = [(i, i + 1) for i in range(size - 1)]
    up = [(i + 1, i) for i in range(size - 1)]
    top = lax.ppermute(cells[:, -1:], axis_name, down)
    bottom = lax.ppermute(cells[:, :1], axis_name, up)
    return jnp.concatenate([top, cells, bottom], axis=1)


def conv_body(x_ref, w_ref, b_ref, *rest):
    step = pl.program_id(0)
    o_ref, acc_ref = rest[-2:]
    rows, cols, outs = o_ref.shape[1:]
    chans = x_ref.shape[-1]
    acc_ref[...] = jnp.broadcast_to(b_ref[...], acc_ref.shape)
    for i in range(3):
        for j in range(3):
            for k in range(3):
                patch = x_ref[step + i, pl.ds(j, rows), pl.ds(k, cols), :]
                acc_ref[...] += jnp.dot(
                    patch.reshape(rows * cols, chans),
                    w_ref[9 * i + 3 * j + k],
                    preferred_element_type=jnp.float32,
                )
    total = acc_ref[...].reshape(rows, cols, outs)
    if len(rest) == 3:
        total = rest[0][0].astype(jnp.float32) + total
    o_ref[0] = total.astype(o_ref.dtype)


def causal_conv(extended, kernel, bias, out_dtype, residual=None):
    leading = jnp.concatenate([extended[:1], extended[:1], extended], axis=0)
    padded = jnp.pad(leading, ((0, 0), (0, 0), (1, 1), (0, 0)))
    frames = extended.shape[0]
    rows = extended.shape[1] - 2
    cols = extended.shape[2]
    taps, chans, outs = kernel.shape
    flops = 2 * frames * rows * cols * chans * outs * taps
    moved = padded.size * 2 + kernel.size * 2 + frames * rows * cols * outs * 4
    in_specs = [
        pl.BlockSpec(padded.shape, lambda t: (0, 0, 0, 0)),
        pl.BlockSpec(kernel.shape, lambda t: (0, 0, 0)),
        pl.BlockSpec((1, outs), lambda t: (0, 0)),
    ]
    operands = [padded, kernel, bias.reshape(1, outs)]
    if residual is not None:
        in_specs.append(pl.BlockSpec((1, rows, cols, outs), lambda t: (t, 0, 0, 0)))
        operands.append(residual)
    return pl.pallas_call(
        conv_body,
        grid=(frames,),
        in_specs=in_specs,
        out_specs=pl.BlockSpec((1, rows, cols, outs), lambda t: (t, 0, 0, 0)),
        out_shape=jax.ShapeDtypeStruct((frames, rows, cols, outs), out_dtype),
        scratch_shapes=[pltpu.VMEM((rows * cols, outs), jnp.float32)],
        cost_estimate=pl.CostEstimate(flops=flops, bytes_accessed=moved, transcendentals=0),
    )(*operands)


def kernel_block(shard, chans):
    size = lax.axis_size("ha") * lax.axis_size("hb")
    me = lax.axis_index(HQ)
    taps, in_block, outs = shard.shape
    width = outs // size
    out = jnp.zeros((taps, in_block * size, width), shard.dtype)
    for step in range(size):
        target = (me + step) % size
        piece = lax.dynamic_slice_in_dim(shard, target * width, width, axis=2)
        if step:
            piece = lax.ppermute(piece, HQ, shift_pairs(size, step))
        source = (me - step) % size
        out = lax.dynamic_update_slice(out, piece, (0, source * in_block, 0))
    return lax.all_gather(out, "hz", axis=1, tiled=True)


def scatter_rows(branch, slab_rows, chans):
    size = lax.axis_size("ha") * lax.axis_size("hb")
    me = lax.axis_index(HQ)
    frames, rows, cols, width = branch.shape
    out = jnp.zeros((frames, slab_rows, cols, chans), branch.dtype)
    for step in range(size):
        target = (me + step) % size
        piece = lax.dynamic_slice_in_dim(branch, target * slab_rows, slab_rows, axis=1)
        if step:
            piece = lax.ppermute(piece, HQ, shift_pairs(size, step))
        source = (me - step) % size
        out = lax.dynamic_update_slice(out, piece, (0, 0, 0, source * width))
    return out


def per_device(
    latent,
    gain_first,
    shift_first,
    kernel_first,
    bias_first,
    gain_second,
    shift_second,
    kernel_second,
    bias_second,
):
    frames, slab_rows, cols, chans = latent.shape
    blocks = lax.axis_size("ha") * lax.axis_size("hb")
    width = chans // blocks
    me = lax.axis_index(HQ)
    group_size = chans // GROUPS

    weights_first = kernel_block(kernel_first, chans)
    weights_second = kernel_block(kernel_second, chans)

    values = latent.astype(jnp.float32)
    sums, squares, count = local_stats(values, GROUPS)
    raw_rows = with_row_halo(chip_gather(latent, 1), "hz")
    sums, squares, count = butterfly_stats(sums, squares, count, ("ha", "hb", "hz"))
    mean_chan, scale_chan = group_scale(sums, squares, count, group_size)
    act_first = activate(raw_rows.astype(jnp.float32), mean_chan, scale_chan, gain_first, shift_first)
    own_bias = lax.dynamic_slice_in_dim(bias_first, me * width, width)
    hidden = causal_conv(edge_mask(act_first), weights_first, own_bias, jnp.bfloat16)

    sums, squares, count = local_stats(hidden.astype(jnp.float32), width // group_size)
    raw_next = chip_gather(with_row_halo(hidden, "hz"), 3)
    sums, squares, count = butterfly_stats(sums, squares, count, ("hz",))
    packed = chip_gather(jnp.stack([sums, squares]), 1)
    mean_chan, scale_chan = group_scale(packed[0], packed[1], count, group_size)
    act_second = activate(raw_next.astype(jnp.float32), mean_chan, scale_chan, gain_second, shift_second)
    own_bias_next = lax.dynamic_slice_in_dim(bias_second, me * width, width)

    own_latent = lax.dynamic_slice_in_dim(raw_rows[:, 1:-1], me * width, width, axis=3)
    summed = causal_conv(
        edge_mask(act_second), weights_second, own_bias_next, jnp.bfloat16, own_latent
    )
    summed_rows = scatter_rows(summed, slab_rows, chans)
    return jnp.repeat(jnp.repeat(summed_rows, 2, axis=1), 2, axis=2)


def solution(mesh):
    groups = mesh.shape["groups"]
    height = mesh.shape["height"]
    blocks = CHAN_BLOCKS
    split = Mesh(
        mesh.devices.reshape(groups, height // blocks, 2, blocks // 2),
        ("groups", "hz", "ha", "hb"),
    )
    rows = ("groups", "hz", "ha", "hb")
    slabs = ("hz", "ha", "hb")
    placed = (
        P(None, rows, None, None),
        P(),
        P(),
        P(None, slabs, None),
        P(),
        P(),
        P(),
        P(None, slabs, None),
        P(),
    )
    return jax.shard_map(
        per_device,
        mesh=split,
        in_specs=placed,
        out_specs=P(None, rows, None, None),
        check_vma=False,
    )
```
